256 devices in a mesh: gx: 4 (over x), gy: 8 (over z_hi, core), gz: 8 (over z_lo, y).
Axes of the slice: x: 4, y: 4, z: 8 (z_hi: 4, z_lo: 2; z = z_hi * 2 + z_lo), core: 2. Of those that a mesh axis runs over, the one named last changes fastest.
Arguments:
- fine: float32 [5, 64, 128, 1024], P(None, 'gx', 'gy', 'gz'), as said below
- shell: float32 [4, 512, 3840], P('gx', ('gy', 'gz')), as said below
- parent: int32 [4, 512], P('gx'), may hold values from 0 to 511, as said below
- link: int32 [6, 4, 8, 64], P(None, 'gx', 'gy', 'gz'), may hold values 0 or 1
Outputs:
- fine_new: float32 [5, 64, 128, 1024], P(None, 'gx', 'gy', 'gz')
- coarse_new: float32 [4, 512, 2560], P('gx', ('gy', 'gz'))
The draws below stay inside these ranges and needn't reach their ends.
Inputs may be any that keep to these rules, and one draw needn't show every extreme that they name: Each row parent[i, :] names every slot 0 to 511 exactly once. Of the 8 blocks q = d * 8 to d * 8 + 7 of a row, at most 2 have parents among the slots o * 8 to o * 8 + 7 of any one o, and every such pair that meets at all holds exactly 2. `fine`: density and energy make pressure positive in every cell; velocities stay well below the sound speed times a few. `shell`: same physical ranges as fine.
All inputs are finite; a program needn't handle non-finite values. No bound on the sum of `link` on one device may be relied on, other than what follows from the above.
Results may differ from the reference program's by a relative error of at most 0.0003.
Values sent between devices are 32-bit elements; how exact they have to be, the bound alone decides.
No kernel may reach another device: no remote copies, remote signals or barrier semaphores. Data moves between devices by JAX's collectives and lax.ppermute only.
A program may use at most 128 MiB of HBM per device.

```python
import jax
import jax.numpy as jnp
from jax import lax

BS = 16
BLK = 8
CAP = 2
NBZ = 64
NQ = 512
NX = 64
NY = 128
NZ = 1024
SHELL = 3840
COARSE = 2560
N_GX = 4
N_GY = 8
N_GZ = 8


def conserved(key, shape):
    keys = jax.random.split(key, 5)
    rho = jnp.exp(jax.random.uniform(keys[0], shape, jnp.float32, jnp.log(0.5), jnp.log(2.0)))
    press = jnp.exp(jax.random.uniform(keys[1], shape, jnp.float32, jnp.log(0.5), jnp.log(2.0)))
    vels = [0.5 * jnp.clip(jax.random.normal(keys[2 + c], shape, jnp.float32), -3.0, 3.0) for c in range(3)]
    kinetic = 0.5 * rho * (vels[0] * vels[0] + vels[1] * vels[1] + vels[2] * vels[2])
    energy = press / 0.4 + kinetic
    return [rho, rho * vels[0], rho * vels[1], rho * vels[2], energy]


def draw_fine(key, part):
    fields = conserved(jax.random.fold_in(key, 11), (NX, NY, NZ))
    return jnp.stack(fields, axis=0).astype(jnp.float32)


def draw_shell(key, part):
    half = BS // 2
    fields = conserved(jax.random.fold_in(key, 23), (N_GX, NQ, 2, 6, half * half))
    stacked = jnp.stack(fields, axis=4)
    return stacked.reshape(N_GX, NQ, SHELL).astype(jnp.float32)


def draw_parent(key, part):
    groups = N_GY * N_GZ
    base = jax.random.fold_in(key, 37)
    result = []
    for row in range(N_GX):
        row_key = jax.random.fold_in(base, row)
        order = jax.random.permutation(jax.random.fold_in(row_key, 1), groups).astype(jnp.int32)
        slot_keys = jax.random.split(jax.random.fold_in(row_key, 2), groups)
        shuffles = jax.vmap(lambda one: jax.random.permutation(one, BLK).astype(jnp.int32))(slot_keys)
        device = jnp.arange(groups, dtype=jnp.int32)[:, None]
        local = jnp.arange(BLK, dtype=jnp.int32)[None, :]
        group = local // CAP
        owner = (order[device] + group) % groups
        within = group * CAP + local % CAP
        placed = shuffles[owner, within]
        result.append((owner * BLK + placed).reshape(NQ))
    return jnp.stack(result, axis=0).astype(jnp.int32)


def with_ends(drawn, own_key, least, high):
    index_at = [jax.random.randint(jax.random.fold_in(own_key, axis), (), 0, length) for axis, length in enumerate(drawn.shape)]
    widest = drawn.shape.index(max(drawn.shape))
    beside = index_at[:widest] + [(index_at[widest] + 1) % drawn.shape[widest]] + index_at[widest + 1:]
    return drawn.at[tuple(index_at)].set(least).at[tuple(beside)].set(high)


def setup_inputs(seed: int = 0) -> dict:
    streams_of = jax.random.split(jax.random.key(seed), 5)
    return {
        "fine": draw_fine(jax.random.fold_in(streams_of[4], 71), 0),
        "shell": draw_shell(jax.random.fold_in(streams_of[4], 71), 0),
        "parent": draw_parent(jax.random.fold_in(streams_of[4], 71), 0),
        "link": with_ends((jax.random.randint(streams_of[3], (6, N_GX, N_GY, NBZ), 0, 3) < 2).astype(jnp.int32), jax.random.fold_in(streams_of[3], 1), 0, 1),
    }


GAMMA = 1.4
LAMBDA = 0.05

def flux_terms(ext, direc):
    rho = ext[:, 0]
    mom = ext[:, 1:4]
    energy = ext[:, 4]
    vel = mom / rho[:, None]
    press = (GAMMA - 1.0) * (energy - 0.5 * lax.optimization_barrier(jnp.sum(mom * vel, axis=1)))
    normal = vel[:, direc]
    parts = [mom[:, direc], mom[:, 0] * normal, mom[:, 1] * normal, mom[:, 2] * normal, (energy + press) * normal]
    parts[1 + direc] = parts[1 + direc] + press
    flux = jnp.stack(parts, axis=1)
    speed = jnp.abs(normal) + jnp.sqrt(GAMMA * press / rho)
    return (flux, speed)

def interface(ext, direc):
    flux, speed = flux_terms(ext, direc)
    dim = 2 + direc
    count = ext.shape[dim]
    f_left = lax.slice_in_dim(flux, 0, count - 1, axis=dim)
    f_right = lax.slice_in_dim(flux, 1, count, axis=dim)
    u_left = lax.slice_in_dim(ext, 0, count - 1, axis=dim)
    u_right = lax.slice_in_dim(ext, 1, count, axis=dim)
    wave = jnp.maximum(lax.slice_in_dim(speed, 0, count - 1, axis=dim - 1), lax.slice_in_dim(speed, 1, count, axis=dim - 1))
    face = 0.5 * (f_left + f_right) - 0.5 * wave[:, None] * (u_right - u_left)
    return lax.slice_in_dim(face, 1, count - 1, axis=dim) - lax.slice_in_dim(face, 0, count - 2, axis=dim)

def advance(core, ghosts):
    ext_x = jnp.concatenate([ghosts[0][:, :, None], core, ghosts[1][:, :, None]], axis=2)
    ext_y = jnp.concatenate([ghosts[2][:, :, :, None], core, ghosts[3][:, :, :, None]], axis=3)
    ext_z = jnp.concatenate([ghosts[4][..., None], core, ghosts[5][..., None]], axis=4)
    total = interface(ext_x, 0) + interface(ext_y, 1) + interface(ext_z, 2)
    return core - LAMBDA * total

def inject(coarse):
    return jnp.repeat(jnp.repeat(coarse, 2, axis=-2), 2, axis=-1)

def mix_ghosts(fine_faces, coarse_faces, links):
    result = []
    for face in range(6):
        chosen = links[:, face][:, None, None, None] == 1
        result.append(jnp.where(chosen, fine_faces[face], inject(coarse_faces[:, face])))
    return result

def restrict(core):
    count = core.shape[0]
    half = core.shape[2] // 2
    grouped = core.reshape(count, 5, half, 2, half, 2, half, 2)
    return grouped.mean(axis=(3, 5, 7)).reshape(count, -1)

def reference(fine, shell, parent, link):
    half = BS // 2
    blocks = fine.reshape(5, N_GX, BS, N_GY, BS, NBZ, BS).transpose(1, 3, 5, 0, 2, 4, 6)
    fetched = jnp.take_along_axis(shell, parent[:, :, None], axis=1)
    fetched = fetched.reshape(N_GX, N_GY, NBZ, 2, 6, 5, half, half)
    level_now = fetched[:, :, :, 0]
    level_mid = 0.5 * (fetched[:, :, :, 0] + fetched[:, :, :, 1])
    links = link.transpose(1, 2, 3, 0)
    rows = N_GX * N_GY
    for step in range(2):
        level = level_now if step == 0 else level_mid
        faces = [jnp.roll(blocks[:, :, :, :, BS - 1], 1, axis=0), jnp.roll(blocks[:, :, :, :, 0], -1, axis=0), jnp.roll(blocks[:, :, :, :, :, BS - 1], 1, axis=1), jnp.roll(blocks[:, :, :, :, :, 0], -1, axis=1), jnp.roll(blocks[..., BS - 1], 1, axis=2), jnp.roll(blocks[..., 0], -1, axis=2)]

        def update(items):
            core, fx0, fx1, fy0, fy1, fz0, fz1, level_row, link_row = items
            ghosts = mix_ghosts([fx0, fx1, fy0, fy1, fz0, fz1], level_row, link_row)
            return advance(core, ghosts)
        packed = tuple((a.reshape((rows, NBZ) + a.shape[3:]) for a in [blocks] + faces + [level, links]))
        blocks = lax.map(update, packed).reshape(blocks.shape)
    restricted = lax.map(restrict, blocks.reshape((rows, NBZ) + blocks.shape[3:]))
    restricted = restricted.reshape(N_GX, NQ, COARSE)
    inverse = jnp.argsort(parent, axis=1).astype(jnp.int32)
    coarse_new = jnp.take_along_axis(restricted, inverse[:, :, None], axis=1)
    fine_new = blocks.transpose(3, 0, 4, 1, 5, 2, 6).reshape(5, NX, NY, NZ)
    return (fine_new, coarse_new)
```

```python
import jax
import jax.numpy as jnp
from jax import lax
from jax.sharding import PartitionSpec as P

BS = 16


GAMMA = 1.4
LAMBDA = 0.05


def padded_2(cells, sides, width):
    for axis, dim in sides:
        count = lax.axis_size(axis)
        head = lax.slice_in_dim(cells, 0, width, axis=dim)
        tail = lax.slice_in_dim(cells, cells.shape[dim] - width, cells.shape[dim], axis=dim)
        cells = jnp.concatenate(
            [
                lax.ppermute(tail, axis, [(i, (i + 1) % count) for i in range(count)]),
                cells,
                lax.ppermute(head, axis, [((i + 1) % count, i) for i in range(count)]),
            ],
            axis=dim,
        )
    return cells


def cell_flux(state, direc):
    rho = state[0]
    mom = state[1:4]
    energy = state[4]
    vel = mom / rho[None]
    press = (GAMMA - 1.0) * (energy - 0.5 * jnp.sum(mom * vel, axis=0))
    normal = vel[direc]
    parts = [
        mom[direc],
        mom[0] * normal,
        mom[1] * normal,
        mom[2] * normal,
        (energy + press) * normal,
    ]
    parts[1 + direc] = parts[1 + direc] + press
    flux = jnp.stack(parts, axis=0)
    speed = jnp.abs(normal) + jnp.sqrt(GAMMA * press / rho)
    return (flux, speed)


def pair_face(flux_a, speed_a, value_a, flux_b, speed_b, value_b):
    return 0.5 * (flux_a + flux_b) - 0.5 * jnp.maximum(speed_a, speed_b)[None] * (value_b - value_a)


def along_axis(ext, direc):
    flux, speed = cell_flux(ext, direc)
    dim = 1 + direc
    count = ext.shape[dim]
    face = pair_face(
        lax.slice_in_dim(flux, 0, count - 1, axis=dim),
        lax.slice_in_dim(speed, 0, count - 1, axis=dim - 1),
        lax.slice_in_dim(ext, 0, count - 1, axis=dim),
        lax.slice_in_dim(flux, 1, count, axis=dim),
        lax.slice_in_dim(speed, 1, count, axis=dim - 1),
        lax.slice_in_dim(ext, 1, count, axis=dim),
    )
    return lax.slice_in_dim(face, 1, count - 1, axis=dim) - lax.slice_in_dim(
        face, 0, count - 2, axis=dim
    )


def along_blocks(state, ghost_low, ghost_high):
    nz_dev = state.shape[3]
    flux, speed = cell_flux(state, 2)
    inner = pair_face(
        jnp.roll(flux, 1, axis=3),
        jnp.roll(speed, 1, axis=2),
        jnp.roll(state, 1, axis=3),
        flux,
        speed,
        state,
    )
    low_flux, low_speed = cell_flux(ghost_low, 2)
    high_flux, high_speed = cell_flux(ghost_high, 2)
    start = pair_face(
        low_flux, low_speed, ghost_low, flux[..., 0::BS], speed[..., 0::BS], state[..., 0::BS]
    )
    finish = pair_face(
        flux[..., BS - 1 :: BS],
        speed[..., BS - 1 :: BS],
        state[..., BS - 1 :: BS],
        high_flux,
        high_speed,
        ghost_high,
    )
    plane = jnp.arange(nz_dev, dtype=jnp.int32) % BS
    left_face = jnp.where(plane == 0, jnp.repeat(start, BS, axis=3), inner)
    right_face = jnp.where(
        plane == BS - 1, jnp.repeat(finish, BS, axis=3), jnp.roll(left_face, -1, axis=3)
    )
    return right_face - left_face


def inject(coarse):
    return jnp.repeat(jnp.repeat(coarse, 2, axis=-2), 2, axis=-1)


def side_ghost(fine_face, level, links, face, nz_dev):
    coarse = inject(level[:, face]).transpose(1, 2, 0, 3).reshape(5, BS, nz_dev)
    chosen = jnp.repeat(links[:, face] == 1, BS)[None, None, :]
    return jnp.where(chosen, fine_face, coarse)


def end_ghost(fine_face, level, links, face):
    coarse = inject(level[:, face]).transpose(1, 2, 3, 0)
    chosen = (links[:, face] == 1)[None, None, None, :]
    return jnp.where(chosen, fine_face, coarse)


def restrict_state(state, nblk):
    half = BS // 2
    grouped = state.reshape(5, half, 2, half, 2, nblk, half, 2)
    means = grouped.mean(axis=(2, 4, 7))
    return means.transpose(3, 0, 1, 2, 4).reshape(nblk, -1)


CAP = 2


def routes(parent_row, nblk):
    ndev = parent_row.shape[0] // nblk
    owner = (parent_row // nblk).reshape(ndev, nblk)
    slot = (parent_row % nblk).reshape(ndev, nblk)
    pos = jnp.arange(nblk, dtype=jnp.int32)
    same = owner[:, :, None] == owner[:, None, :]
    earlier = (pos[None, :] < pos[:, None])[None]
    rank = jnp.sum((same & earlier).astype(jnp.int32), axis=2)
    return owner, slot, rank


def shards(fine, shell, parent, link):
    half = BS // 2
    nz_dev = fine.shape[3]
    nblk = nz_dev // BS
    me = lax.axis_index("gy") * lax.axis_size("gz") + lax.axis_index("gz")
    parent_row = parent[0]
    ndev = parent_row.shape[0] // nblk
    links = link[:, 0, 0, :].T
    width = shell.shape[2] // 2
    owner, slot, rank = routes(parent_row, nblk)

    mine = owner == me
    picks = jnp.stack(
        [jnp.sum(jnp.where(mine & (rank == c), slot, 0), axis=1) for c in range(CAP)], axis=1
    )
    local = shell[0]
    levels = jnp.concatenate(
        [local[:, :width], 0.5 * (local[:, :width] + local[:, width:])], axis=1
    )
    outgoing = jnp.take(levels, picks.reshape(-1), axis=0, mode="clip").reshape(
        ndev, CAP, levels.shape[1]
    )
    incoming = lax.all_to_all(outgoing, ("gy", "gz"), 0, 0, tiled=True)
    my_owner = lax.dynamic_index_in_dim(owner, me, keepdims=False)
    my_rank = lax.dynamic_index_in_dim(rank, me, keepdims=False)
    fetched = jnp.take(
        incoming.reshape(ndev * CAP, -1), my_owner * CAP + my_rank, axis=0, mode="clip"
    )
    level_now = fetched[:, :width]
    level_mid = fetched[:, width:]
    state = fine
    for step in range(2):
        level = (level_now if step == 0 else level_mid).reshape(nblk, 6, 5, half, half)
        padded = padded_2(state, (("gx", 1), ("gy", 2), ("gz", 3)), 1)
        ghost_x0 = side_ghost(padded[:, 0, 1:-1, 1:-1], level, links, 0, nz_dev)
        ghost_x1 = side_ghost(padded[:, -1, 1:-1, 1:-1], level, links, 1, nz_dev)
        ghost_y0 = side_ghost(padded[:, 1:-1, 0, 1:-1], level, links, 2, nz_dev)
        ghost_y1 = side_ghost(padded[:, 1:-1, -1, 1:-1], level, links, 3, nz_dev)
        ghost_z0 = end_ghost(padded[:, 1:-1, 1:-1, 0:nz_dev:BS], level, links, 4)
        ghost_z1 = end_ghost(padded[:, 1:-1, 1:-1, BS + 1 :: BS], level, links, 5)
        ext_x = jnp.concatenate([ghost_x0[:, None], state, ghost_x1[:, None]], axis=1)
        ext_y = jnp.concatenate([ghost_y0[:, :, None], state, ghost_y1[:, :, None]], axis=2)
        total = (
            along_axis(ext_x, 0) + along_axis(ext_y, 1) + along_blocks(state, ghost_z0, ghost_z1)
        )
        state = state - LAMBDA * total
    restricted = restrict_state(state, nblk)

    pos = jnp.arange(nblk, dtype=jnp.int32)
    dest = jnp.arange(ndev, dtype=jnp.int32)[:, None, None]
    cell = jnp.arange(CAP, dtype=jnp.int32)[None, :, None]
    hit = (my_owner[None, None, :] == dest) & (my_rank[None, None, :] == cell)
    which = jnp.sum(jnp.where(hit, pos[None, None, :], 0), axis=2)
    back = jnp.take(restricted, which.reshape(-1), axis=0, mode="clip").reshape(
        ndev, CAP, restricted.shape[1]
    )
    returned = lax.all_to_all(back, ("gy", "gz"), 0, 0, tiled=True)
    target = me * nblk + pos
    source = (jnp.arange(ndev * nblk, dtype=jnp.int32) // nblk) * CAP + rank.reshape(-1)
    match = parent_row[None, :] == target[:, None]
    origin = jnp.sum(jnp.where(match, source[None, :], 0), axis=1)
    gathered = jnp.take(returned.reshape(ndev * CAP, -1), origin, axis=0, mode="clip")
    coarse_new = gathered.reshape(1, nblk, restricted.shape[1])
    return (state, coarse_new)


def solution(mesh):
    return jax.shard_map(
        shards,
        mesh=mesh,
        in_specs=(
            P(None, "gx", "gy", "gz"),
            P("gx", ("gy", "gz"), None),
            P("gx", None),
            P(None, "gx", "gy", "gz"),
        ),
        out_specs=(P(None, "gx", "gy", "gz"), P("gx", ("gy", "gz"), None)),
        check_vma=False,
    )
```

```python
import jax
import jax.numpy as jnp
from jax import lax
from jax.experimental import pallas as pl
from jax.experimental.pallas import tpu as pltpu
from jax.sharding import PartitionSpec as P

BS = 16
CAP = 2

GAMMA = 1.4
LAMBDA = 0.05


def shift_in(plane, axis, forward):
    count = lax.axis_size(axis)
    if forward:
        pairs = [(i, (i + 1) % count) for i in range(count)]
    else:
        pairs = [((i + 1) % count, i) for i in range(count)]
    return lax.ppermute(plane, axis, pairs)


def prims(v):
    rho, mx, my, mz, energy = v
    ux = mx / rho
    uy = my / rho
    uz = mz / rho
    press = (GAMMA - 1.0) * (energy - 0.5 * (mx * ux + my * uy + mz * uz))
    sound = jnp.sqrt(GAMMA * press / rho)
    return (ux, uy, uz), press, sound


def flux_of(v, prim, direc):
    rho, mx, my, mz, energy = v
    vel, press, sound = prim
    normal = vel[direc]
    mom = (mx, my, mz)
    parts = [mom[direc], mx * normal, my * normal, mz * normal, (energy + press) * normal]
    parts[1 + direc] = parts[1 + direc] + press
    return parts, jnp.abs(normal) + sound


def face_of(fa, sa, va, fb, sb, vb):
    wave = 0.5 * jnp.maximum(sa, sb)
    return [0.5 * (fa[i] + fb[i]) - wave * (vb[i] - va[i]) for i in range(5)]


def substep_kernel(u_ref, gx_ref, gy_ref, zfix_ref, zflag_ref, o_ref):
    nx = u_ref.shape[1]
    ny = u_ref.shape[2]
    nz = u_ref.shape[3]
    row = lax.broadcasted_iota(jnp.int32, (ny, nz), 0)
    over_lo = zflag_ref[0] != 0
    over_hi = zflag_ref[1] != 0

    def body(x, carry):
        cen = [u_ref[f, x] for f in range(5)]
        below = jnp.maximum(x - 1, 0)
        above = jnp.minimum(x + 1, nx - 1)
        xm = [jnp.where(x == 0, gx_ref[0, f], u_ref[f, below]) for f in range(5)]
        xp = [jnp.where(x == nx - 1, gx_ref[1, f], u_ref[f, above]) for f in range(5)]
        ym = [
            jnp.where(row == 0, jnp.broadcast_to(gy_ref[0, x, f], (ny, nz)), pltpu.roll(cen[f], 1, 0))
            for f in range(5)
        ]
        yp = [
            jnp.where(
                row == ny - 1, jnp.broadcast_to(gy_ref[1, x, f], (ny, nz)), pltpu.roll(cen[f], ny - 1, 0)
            )
            for f in range(5)
        ]
        zm = [jnp.where(over_lo, zfix_ref[f, x], pltpu.roll(cen[f], 1, 1)) for f in range(5)]
        zp = [jnp.where(over_hi, zfix_ref[f, x], pltpu.roll(cen[f], nz - 1, 1)) for f in range(5)]
        pc = prims(cen)
        total = None
        for direc, (lo, hi) in enumerate(((xm, xp), (ym, yp), (zm, zp))):
            fc, sc = flux_of(cen, pc, direc)
            fl, sl = flux_of(lo, prims(lo), direc)
            fh, sh = flux_of(hi, prims(hi), direc)
            left = face_of(fl, sl, lo, fc, sc, cen)
            right = face_of(fc, sc, cen, fh, sh, hi)
            diff = [right[i] - left[i] for i in range(5)]
            total = diff if total is None else [total[i] + diff[i] for i in range(5)]
        for f in range(5):
            o_ref[f, x] = cen[f] - LAMBDA * total[f]
        return carry

    lax.fori_loop(0, nx, body, 0)


def substep(state, gx, gy, zfix, zflag):
    return pl.pallas_call(
        substep_kernel, out_shape=jax.ShapeDtypeStruct(state.shape, state.dtype)
    )(state, gx, gy, zfix, zflag)


def inject(coarse):
    return jnp.repeat(jnp.repeat(coarse, 2, axis=-2), 2, axis=-1)


def side_ghost(fine_face, level, links, face, nz_dev):
    coarse = inject(level[:, face]).transpose(1, 2, 0, 3).reshape(5, BS, nz_dev)
    chosen = jnp.repeat(links[:, face] == 1, BS)[None, None, :]
    return jnp.where(chosen, fine_face, coarse)


def ghost_inputs(state, level, links):
    nz_dev = state.shape[3]
    gx = jnp.stack(
        [
            side_ghost(shift_in(state[:, -1], "gx", True), level, links, 0, nz_dev),
            side_ghost(shift_in(state[:, 0], "gx", False), level, links, 1, nz_dev),
        ]
    )
    gy = jnp.stack(
        [
            side_ghost(shift_in(state[:, :, -1], "gy", True), level, links, 2, nz_dev),
            side_ghost(shift_in(state[:, :, 0], "gy", False), level, links, 3, nz_dev),
        ]
    )
    gy = gy.transpose(0, 2, 1, 3)[:, :, :, None, :]
    far_lo = shift_in(state[..., -1], "gz", True)
    far_hi = shift_in(state[..., 0], "gz", False)
    lane = jnp.arange(nz_dev, dtype=jnp.int32)
    at_lo = lane % BS == 0
    at_hi = lane % BS == BS - 1
    link_lo = jnp.repeat(links[:, 4] == 1, BS)
    link_hi = jnp.repeat(links[:, 5] == 1, BS)
    coarse_lo = jnp.repeat(inject(level[:, 4]).transpose(1, 2, 3, 0), BS, axis=3)
    coarse_hi = jnp.repeat(inject(level[:, 5]).transpose(1, 2, 3, 0), BS, axis=3)
    lo_val = jnp.where(link_lo & (lane == 0), far_lo[..., None], coarse_lo)
    hi_val = jnp.where(link_hi & (lane == nz_dev - 1), far_hi[..., None], coarse_hi)
    zfix = jnp.where(at_lo, lo_val, hi_val)
    flag_lo = at_lo & (~link_lo | (lane == 0))
    flag_hi = at_hi & (~link_hi | (lane == nz_dev - 1))
    zflag = jnp.broadcast_to(
        jnp.stack([flag_lo, flag_hi]).astype(jnp.int32)[:, None, :], (2, state.shape[2], nz_dev)
    )
    return gx, gy, zfix, zflag


def restrict_state(state, nblk):
    half = BS // 2
    grouped = state.reshape(5, half, 2, half, 2, nblk, half, 2)
    means = grouped.mean(axis=(2, 4, 7))
    return means.transpose(3, 0, 1, 2, 4).reshape(nblk, -1)


def routes(parent_row, nblk):
    ndev = parent_row.shape[0] // nblk
    owner = (parent_row // nblk).reshape(ndev, nblk)
    slot = (parent_row % nblk).reshape(ndev, nblk)
    pos = jnp.arange(nblk, dtype=jnp.int32)
    same = owner[:, :, None] == owner[:, None, :]
    earlier = (pos[None, :] < pos[:, None])[None]
    rank = jnp.sum((same & earlier).astype(jnp.int32), axis=2)
    return owner, slot, rank


def shards(fine, shell, parent, link):
    half = BS // 2
    nz_dev = fine.shape[3]
    nblk = nz_dev // BS
    me = lax.axis_index("gy") * lax.axis_size("gz") + lax.axis_index("gz")
    parent_row = parent[0]
    ndev = parent_row.shape[0] // nblk
    links = link[:, 0, 0, :].T
    width = shell.shape[2] // 2
    owner, slot, rank = routes(parent_row, nblk)

    mine = owner == me
    picks = jnp.stack(
        [jnp.sum(jnp.where(mine & (rank == c), slot, 0), axis=1) for c in range(CAP)], axis=1
    )
    local = shell[0]
    levels = jnp.concatenate(
        [local[:, :width], 0.5 * (local[:, :width] + local[:, width:])], axis=1
    )
    outgoing = jnp.take(levels, picks.reshape(-1), axis=0, mode="clip").reshape(
        ndev, CAP, levels.shape[1]
    )
    incoming = lax.all_to_all(outgoing, ("gy", "gz"), 0, 0, tiled=True)
    my_owner = lax.dynamic_index_in_dim(owner, me, keepdims=False)
    my_rank = lax.dynamic_index_in_dim(rank, me, keepdims=False)
    fetched = jnp.take(
        incoming.reshape(ndev * CAP, -1), my_owner * CAP + my_rank, axis=0, mode="clip"
    )
    level_now = fetched[:, :width]
    level_mid = fetched[:, width:]
    state = fine
    for step in range(2):
        level = (level_now if step == 0 else level_mid).reshape(nblk, 6, 5, half, half)
        state = substep(state, *ghost_inputs(state, level, links))
    restricted = restrict_state(state, nblk)

    pos = jnp.arange(nblk, dtype=jnp.int32)
    dest = jnp.arange(ndev, dtype=jnp.int32)[:, None, None]
    cell = jnp.arange(CAP, dtype=jnp.int32)[None, :, None]
    hit = (my_owner[None, None, :] == dest) & (my_rank[None, None, :] == cell)
    which = jnp.sum(jnp.where(hit, pos[None, None, :], 0), axis=2)
    back = jnp.take(restricted, which.reshape(-1), axis=0, mode="clip").reshape(
        ndev, CAP, restricted.shape[1]
    )
    returned = lax.all_to_all(back, ("gy", "gz"), 0, 0, tiled=True)
    target = me * nblk + pos
    source = (jnp.arange(ndev * nblk, dtype=jnp.int32) // nblk) * CAP + rank.reshape(-1)
    match = parent_row[None, :] == target[:, None]
    origin = jnp.sum(jnp.where(match, source[None, :], 0), axis=1)
    gathered = jnp.take(returned.reshape(ndev * CAP, -1), origin, axis=0, mode="clip")
    coarse_new = gathered.reshape(1, nblk, restricted.shape[1])
    return (state, coarse_new)


def solution(mesh):
    return jax.shard_map(
        shards,
        mesh=mesh,
        in_specs=(
            P(None, "gx", "gy", "gz"),
            P("gx", ("gy", "gz"), None),
            P("gx", None),
            P(None, "gx", "gy", "gz"),
        ),
        out_specs=(P(None, "gx", "gy", "gz"), P("gx", ("gy", "gz"), None)),
        check_vma=False,
    )
```

```python
import jax
import jax.numpy as jnp
from jax import lax
from jax.experimental import pallas as pl
from jax.experimental.pallas import tpu as pltpu
from jax.sharding import PartitionSpec as P

BS = 16
CAP = 2

GAMMA = 1.4
LAMBDA = 0.05


def shift_in(plane, axis, forward):
    count = lax.axis_size(axis)
    if forward:
        pairs = [(i, (i + 1) % count) for i in range(count)]
    else:
        pairs = [((i + 1) % count, i) for i in range(count)]
    return lax.ppermute(plane, axis, pairs)


def prims(v):
    rho, mx, my, mz, energy = v
    ux = mx / rho
    uy = my / rho
    uz = mz / rho
    press = (GAMMA - 1.0) * (energy - 0.5 * (mx * ux + my * uy + mz * uz))
    sound = jnp.sqrt(GAMMA * press / rho)
    return (ux, uy, uz), press, sound


def flux_of(v, prim, direc):
    rho, mx, my, mz, energy = v
    vel, press, sound = prim
    normal = vel[direc]
    mom = (mx, my, mz)
    parts = [mom[direc], mx * normal, my * normal, mz * normal, (energy + press) * normal]
    parts[1 + direc] = parts[1 + direc] + press
    return parts, jnp.abs(normal) + sound


def face_of(fa, sa, va, fb, sb, vb):
    wave = 0.5 * jnp.maximum(sa, sb)
    return [0.5 * (fa[i] + fb[i]) - wave * (vb[i] - va[i]) for i in range(5)]


def substep_kernel(u_ref, gx_ref, gy_ref, zfix_ref, zflag_ref, o_ref):
    nx = u_ref.shape[1]
    ny = u_ref.shape[2]
    nz = u_ref.shape[3]
    row = lax.broadcasted_iota(jnp.int32, (ny, nz), 0)
    over_lo = zflag_ref[0] != 0
    over_hi = zflag_ref[1] != 0

    def body(x, carry):
        cen = [u_ref[f, x] for f in range(5)]
        below = jnp.maximum(x - 1, 0)
        above = jnp.minimum(x + 1, nx - 1)
        xm = [jnp.where(x == 0, gx_ref[0, f], u_ref[f, below]) for f in range(5)]
        xp = [jnp.where(x == nx - 1, gx_ref[1, f], u_ref[f, above]) for f in range(5)]
        ym = [
            jnp.where(row == 0, jnp.broadcast_to(gy_ref[0, x, f], (ny, nz)), pltpu.roll(cen[f], 1, 0))
            for f in range(5)
        ]
        yp = [
            jnp.where(
                row == ny - 1, jnp.broadcast_to(gy_ref[1, x, f], (ny, nz)), pltpu.roll(cen[f], ny - 1, 0)
            )
            for f in range(5)
        ]
        zm = [jnp.where(over_lo, zfix_ref[f, x], pltpu.roll(cen[f], 1, 1)) for f in range(5)]
        zp = [jnp.where(over_hi, zfix_ref[f, x], pltpu.roll(cen[f], nz - 1, 1)) for f in range(5)]
        pc = prims(cen)
        total = None
        for direc, (lo, hi) in enumerate(((xm, xp), (ym, yp), (zm, zp))):
            fc, sc = flux_of(cen, pc, direc)
            fl, sl = flux_of(lo, prims(lo), direc)
            fh, sh = flux_of(hi, prims(hi), direc)
            left = face_of(fl, sl, lo, fc, sc, cen)
            right = face_of(fc, sc, cen, fh, sh, hi)
            diff = [right[i] - left[i] for i in range(5)]
            total = diff if total is None else [total[i] + diff[i] for i in range(5)]
        for f in range(5):
            o_ref[f, x] = cen[f] - LAMBDA * total[f]
        return carry

    lax.fori_loop(0, nx, body, 0)


def substep(state, gx, gy, zfix, zflag):
    return pl.pallas_call(
        substep_kernel, out_shape=jax.ShapeDtypeStruct(state.shape, state.dtype)
    )(state, gx, gy, zfix, zflag)


def replicate(rows, cols):
    step = cols // rows
    return (jnp.arange(cols)[None, :] // step == jnp.arange(rows)[:, None]).astype(jnp.float32)


def exact_dot(spec, *ops):
    return jnp.einsum(spec, *ops, precision=lax.Precision.HIGHEST, preferred_element_type=jnp.float32)


def coarse_faces(fetched, nblk):
    half = BS // 2
    lv = fetched.reshape(nblk, 2, 6, 5, half, half)
    rows = replicate(half, BS)
    side = lv[:, :, 0:4].transpose(1, 2, 3, 4, 0, 5).reshape(2, 4, 5, half, nblk * half)
    side = exact_dot("ay,lkfab,bz->lkfyz", rows, side, replicate(nblk * half, nblk * BS))
    ends = lv[:, :, 4:6].transpose(1, 2, 3, 4, 5, 0)
    ends = exact_dot("ax,by,lkfabc,cz->lkfxyz", rows, rows, ends, replicate(nblk, nblk * BS))
    return side, ends


def ghost_inputs(state, side, ends, links):
    nz_dev = state.shape[3]
    chosen = [jnp.repeat(links[:, face] == 1, BS)[None, None, :] for face in range(4)]
    gx = jnp.stack(
        [
            jnp.where(chosen[0], shift_in(state[:, -1], "gx", True), side[0]),
            jnp.where(chosen[1], shift_in(state[:, 0], "gx", False), side[1]),
        ]
    )
    gy = jnp.stack(
        [
            jnp.where(chosen[2], shift_in(state[:, :, -1], "gy", True), side[2]),
            jnp.where(chosen[3], shift_in(state[:, :, 0], "gy", False), side[3]),
        ]
    )
    gy = gy.transpose(0, 2, 1, 3)[:, :, :, None, :]
    far_lo = shift_in(state[..., -1], "gz", True)
    far_hi = shift_in(state[..., 0], "gz", False)
    lane = jnp.arange(nz_dev, dtype=jnp.int32)
    at_lo = lane % BS == 0
    at_hi = lane % BS == BS - 1
    link_lo = jnp.repeat(links[:, 4] == 1, BS)
    link_hi = jnp.repeat(links[:, 5] == 1, BS)
    lo_val = jnp.where(link_lo & (lane == 0), far_lo[..., None], ends[0])
    hi_val = jnp.where(link_hi & (lane == nz_dev - 1), far_hi[..., None], ends[1])
    zfix = jnp.where(at_lo, lo_val, hi_val)
    flag_lo = at_lo & (~link_lo | (lane == 0))
    flag_hi = at_hi & (~link_hi | (lane == nz_dev - 1))
    zflag = jnp.broadcast_to(
        jnp.stack([flag_lo, flag_hi]).astype(jnp.int32)[:, None, :], (2, state.shape[2], nz_dev)
    )
    return gx, gy, zfix, zflag


def restrict_state(state, nblk):
    half = BS // 2
    nz_dev = state.shape[3]
    pairs = state.reshape(5, half, 2, BS, nz_dev)
    planes = pairs[:, :, 0] + pairs[:, :, 1]
    means = 0.125 * exact_dot(
        "ay,fxyl,lm->fxam", replicate(half, BS), planes, replicate(nblk * half, nz_dev).T
    )
    means = means.reshape(5, half, half, nblk, half)
    return means.transpose(3, 0, 1, 2, 4).reshape(nblk, -1)


def routes(parent_row, nblk):
    ndev = parent_row.shape[0] // nblk
    owner = (parent_row // nblk).reshape(ndev, nblk)
    slot = (parent_row % nblk).reshape(ndev, nblk)
    pos = jnp.arange(nblk, dtype=jnp.int32)
    same = owner[:, :, None] == owner[:, None, :]
    earlier = (pos[None, :] < pos[:, None])[None]
    rank = jnp.sum((same & earlier).astype(jnp.int32), axis=2)
    return owner, slot, rank


def shards(fine, shell, parent, link):
    half = BS // 2
    nz_dev = fine.shape[3]
    nblk = nz_dev // BS
    me = lax.axis_index("gy") * lax.axis_size("gz") + lax.axis_index("gz")
    parent_row = parent[0]
    ndev = parent_row.shape[0] // nblk
    links = link[:, 0, 0, :].T
    width = shell.shape[2] // 2
    owner, slot, rank = routes(parent_row, nblk)

    mine = owner == me
    picks = jnp.stack(
        [jnp.sum(jnp.where(mine & (rank == c), slot, 0), axis=1) for c in range(CAP)], axis=1
    )
    local = shell[0]
    levels = jnp.concatenate(
        [local[:, :width], 0.5 * (local[:, :width] + local[:, width:])], axis=1
    )
    outgoing = jnp.take(levels, picks.reshape(-1), axis=0, mode="clip").reshape(
        ndev, CAP, levels.shape[1]
    )
    incoming = lax.all_to_all(outgoing, ("gy", "gz"), 0, 0, tiled=True)
    my_owner = lax.dynamic_index_in_dim(owner, me, keepdims=False)
    my_rank = lax.dynamic_index_in_dim(rank, me, keepdims=False)
    fetched = jnp.take(
        incoming.reshape(ndev * CAP, -1), my_owner * CAP + my_rank, axis=0, mode="clip"
    )
    side, ends = coarse_faces(fetched, nblk)
    state = fine
    for step in range(2):
        state = substep(state, *ghost_inputs(state, side[step], ends[step], links))
    restricted = restrict_state(state, nblk)

    pos = jnp.arange(nblk, dtype=jnp.int32)
    dest = jnp.arange(ndev, dtype=jnp.int32)[:, None, None]
    cell = jnp.arange(CAP, dtype=jnp.int32)[None, :, None]
    hit = (my_owner[None, None, :] == dest) & (my_rank[None, None, :] == cell)
    which = jnp.sum(jnp.where(hit, pos[None, None, :], 0), axis=2)
    back = jnp.take(restricted, which.reshape(-1), axis=0, mode="clip").reshape(
        ndev, CAP, restricted.shape[1]
    )
    returned = lax.all_to_all(back, ("gy", "gz"), 0, 0, tiled=True)
    target = me * nblk + pos
    source = (jnp.arange(ndev * nblk, dtype=jnp.int32) // nblk) * CAP + rank.reshape(-1)
    match = parent_row[None, :] == target[:, None]
    origin = jnp.sum(jnp.where(match, source[None, :], 0), axis=1)
    gathered = jnp.take(returned.reshape(ndev * CAP, -1), origin, axis=0, mode="clip")
    coarse_new = gathered.reshape(1, nblk, restricted.shape[1])
    return (state, coarse_new)


def solution(mesh):
    return jax.shard_map(
        shards,
        mesh=mesh,
        in_specs=(
            P(None, "gx", "gy", "gz"),
            P("gx", ("gy", "gz"), None),
            P("gx", None),
            P(None, "gx", "gy", "gz"),
        ),
        out_specs=(P(None, "gx", "gy", "gz"), P("gx", ("gy", "gz"), None)),
        check_vma=False,
    )
```

```python
import jax
import jax.numpy as jnp
from jax import lax
from jax.experimental import pallas as pl
from jax.experimental.pallas import tpu as pltpu
from jax.sharding import PartitionSpec as P

BS = 16

GAMMA = 1.4
LAMBDA = 0.05


def shift_in(plane, axis, forward):
    count = lax.axis_size(axis)
    if forward:
        pairs = [(i, (i + 1) % count) for i in range(count)]
    else:
        pairs = [((i + 1) % count, i) for i in range(count)]
    return lax.ppermute(plane, axis, pairs)


def prims(v):
    rho, mx, my, mz, energy = v
    ux = mx / rho
    uy = my / rho
    uz = mz / rho
    press = (GAMMA - 1.0) * (energy - 0.5 * (mx * ux + my * uy + mz * uz))
    sound = jnp.sqrt(GAMMA * press / rho)
    return (ux, uy, uz), press, sound


def flux_of(v, prim, direc):
    rho, mx, my, mz, energy = v
    vel, press, sound = prim
    normal = vel[direc]
    mom = (mx, my, mz)
    parts = [mom[direc], mx * normal, my * normal, mz * normal, (energy + press) * normal]
    parts[1 + direc] = parts[1 + direc] + press
    return parts, jnp.abs(normal) + sound


def face_of(fa, sa, va, fb, sb, vb):
    wave = 0.5 * jnp.maximum(sa, sb)
    return [0.5 * (fa[i] + fb[i]) - wave * (vb[i] - va[i]) for i in range(5)]


def substep_kernel(u_ref, gx_ref, gy_ref, zfix_ref, zflag_ref, o_ref):
    nx = u_ref.shape[1]
    ny = u_ref.shape[2]
    nz = u_ref.shape[3]
    row = lax.broadcasted_iota(jnp.int32, (ny, nz), 0)
    over_lo = zflag_ref[0] != 0
    over_hi = zflag_ref[1] != 0

    def body(x, carry):
        cen = [u_ref[f, x] for f in range(5)]
        below = jnp.maximum(x - 1, 0)
        above = jnp.minimum(x + 1, nx - 1)
        xm = [jnp.where(x == 0, gx_ref[0, f], u_ref[f, below]) for f in range(5)]
        xp = [jnp.where(x == nx - 1, gx_ref[1, f], u_ref[f, above]) for f in range(5)]
        ym = [
            jnp.where(row == 0, jnp.broadcast_to(gy_ref[0, x, f], (ny, nz)), pltpu.roll(cen[f], 1, 0))
            for f in range(5)
        ]
        yp = [
            jnp.where(
                row == ny - 1, jnp.broadcast_to(gy_ref[1, x, f], (ny, nz)), pltpu.roll(cen[f], ny - 1, 0)
            )
            for f in range(5)
        ]
        zm = [jnp.where(over_lo, zfix_ref[f, x], pltpu.roll(cen[f], 1, 1)) for f in range(5)]
        zp = [jnp.where(over_hi, zfix_ref[f, x], pltpu.roll(cen[f], nz - 1, 1)) for f in range(5)]
        pc = prims(cen)
        total = None
        for direc, (lo, hi) in enumerate(((xm, xp), (ym, yp), (zm, zp))):
            fc, sc = flux_of(cen, pc, direc)
            fl, sl = flux_of(lo, prims(lo), direc)
            fh, sh = flux_of(hi, prims(hi), direc)
            left = face_of(fl, sl, lo, fc, sc, cen)
            right = face_of(fc, sc, cen, fh, sh, hi)
            diff = [right[i] - left[i] for i in range(5)]
            total = diff if total is None else [total[i] + diff[i] for i in range(5)]
        for f in range(5):
            o_ref[f, x] = cen[f] - LAMBDA * total[f]
        return carry

    lax.fori_loop(0, nx, body, 0)


def substep(state, gx, gy, zfix, zflag):
    return pl.pallas_call(
        substep_kernel, out_shape=jax.ShapeDtypeStruct(state.shape, state.dtype)
    )(state, gx, gy, zfix, zflag)


def replicate(rows, cols):
    step = cols // rows
    return (jnp.arange(cols)[None, :] // step == jnp.arange(rows)[:, None]).astype(jnp.float32)


def exact_dot(spec, *ops):
    return jnp.einsum(spec, *ops, precision=lax.Precision.HIGHEST, preferred_element_type=jnp.float32)


def coarse_faces(fetched, nblk):
    half = BS // 2
    lv = fetched.reshape(nblk, 2, 6, 5, half, half)
    rows = replicate(half, BS)
    side = lv[:, :, 0:4].transpose(1, 2, 3, 4, 0, 5).reshape(2, 4, 5, half, nblk * half)
    side = exact_dot("ay,lkfab,bz->lkfyz", rows, side, replicate(nblk * half, nblk * BS))
    ends = lv[:, :, 4:6].transpose(1, 2, 3, 4, 5, 0)
    ends = exact_dot("ax,by,lkfabc,cz->lkfxyz", rows, rows, ends, replicate(nblk, nblk * BS))
    return side, ends


def ghost_inputs(state, side, ends, links):
    nz_dev = state.shape[3]
    chosen = [jnp.repeat(links[:, face] == 1, BS)[None, None, :] for face in range(4)]
    gx = jnp.stack(
        [
            jnp.where(chosen[0], shift_in(state[:, -1], "gx", True), side[0]),
            jnp.where(chosen[1], shift_in(state[:, 0], "gx", False), side[1]),
        ]
    )
    gy = jnp.stack(
        [
            jnp.where(chosen[2], shift_in(state[:, :, -1], "gy", True), side[2]),
            jnp.where(chosen[3], shift_in(state[:, :, 0], "gy", False), side[3]),
        ]
    )
    gy = gy.transpose(0, 2, 1, 3)[:, :, :, None, :]
    far_lo = shift_in(state[..., -1], "gz", True)
    far_hi = shift_in(state[..., 0], "gz", False)
    lane = jnp.arange(nz_dev, dtype=jnp.int32)
    at_lo = lane % BS == 0
    at_hi = lane % BS == BS - 1
    link_lo = jnp.repeat(links[:, 4] == 1, BS)
    link_hi = jnp.repeat(links[:, 5] == 1, BS)
    lo_val = jnp.where(link_lo & (lane == 0), far_lo[..., None], ends[0])
    hi_val = jnp.where(link_hi & (lane == nz_dev - 1), far_hi[..., None], ends[1])
    zfix = jnp.where(at_lo, lo_val, hi_val)
    flag_lo = at_lo & (~link_lo | (lane == 0))
    flag_hi = at_hi & (~link_hi | (lane == nz_dev - 1))
    zflag = jnp.broadcast_to(
        jnp.stack([flag_lo, flag_hi]).astype(jnp.int32)[:, None, :], (2, state.shape[2], nz_dev)
    )
    return gx, gy, zfix, zflag


def restrict_state(state, nblk):
    half = BS // 2
    nz_dev = state.shape[3]
    pairs = state.reshape(5, half, 2, BS, nz_dev)
    planes = pairs[:, :, 0] + pairs[:, :, 1]
    means = 0.125 * exact_dot(
        "ay,fxyl,lm->fxam", replicate(half, BS), planes, replicate(nblk * half, nz_dev).T
    )
    means = means.reshape(5, half, half, nblk, half)
    return means.transpose(3, 0, 1, 2, 4).reshape(nblk, -1)


def pick(table, index):
    flat = table.reshape((-1,) + table.shape[2:])
    return jnp.take(flat, index.reshape(-1), axis=0, mode="clip").reshape(
        index.shape + table.shape[2:]
    )


def select(mask, value):
    return jnp.sum(jnp.where(mask, value, 0), axis=-1)


def shards(fine, shell, parent, link):
    nz_dev = fine.shape[3]
    nblk = nz_dev // BS
    rows = lax.axis_size("gy")
    cols = lax.axis_size("gz")
    my = lax.axis_index("gy")
    mz = lax.axis_index("gz")
    me = my * cols + mz
    parent_row = parent[0]
    count = parent_row.shape[0]
    links = link[:, 0, 0, :].T
    width = shell.shape[2] // 2

    item = jnp.arange(count, dtype=jnp.int32)
    dev = item // nblk
    d_row = dev // cols
    d_col = dev % cols
    owner = parent_row // nblk
    slot = parent_row % nblk
    o_row = owner // cols
    o_col = owner % cols
    before = item[None, :] < item[:, None]
    rank1 = jnp.sum(
        (before & (owner[None, :] == owner[:, None]) & (d_row[None, :] == d_row[:, None])).astype(
            jnp.int32
        ),
        axis=1,
    )
    rank2 = jnp.sum(
        (before & (dev[None, :] == dev[:, None]) & (o_col[None, :] == o_col[:, None])).astype(
            jnp.int32
        ),
        axis=1,
    )
    peer_r = jnp.arange(rows, dtype=jnp.int32)[:, None, None]
    peer_c = jnp.arange(cols, dtype=jnp.int32)[:, None, None]
    cell = jnp.arange(nblk, dtype=jnp.int32)[None, :, None]
    via_me = (d_row == my) & (o_col == mz)

    local = shell[0]
    levels = jnp.concatenate(
        [local[:, :width], 0.5 * (local[:, :width] + local[:, width:])], axis=1
    )
    first = select((owner == me) & (d_row == peer_r) & (rank1 == cell), slot)
    stage = lax.all_to_all(pick(levels[None], first), "gy", 0, 0, tiled=True)
    second = select(via_me & (d_col == peer_c) & (rank2 == cell), o_row * nblk + rank1)
    stage = lax.all_to_all(pick(stage, second), "gz", 0, 0, tiled=True)
    mine = lax.dynamic_slice_in_dim(item, me * nblk, nblk)
    fetched = pick(stage, o_col[mine] * nblk + rank2[mine])

    side, ends = coarse_faces(fetched, nblk)
    state = fine
    for step in range(2):
        state = substep(state, *ghost_inputs(state, side[step], ends[step], links))
    restricted = restrict_state(state, nblk)

    pos = jnp.arange(nblk, dtype=jnp.int32)
    back = select(
        (o_col[mine][None, None, :] == peer_c) & (rank2[mine][None, None, :] == cell), pos
    )
    stage = lax.all_to_all(pick(restricted[None], back), "gz", 0, 0, tiled=True)
    home = select(via_me & (o_row == peer_r) & (rank1 == cell), d_col * nblk + rank2)
    stage = lax.all_to_all(pick(stage, home), "gy", 0, 0, tiled=True)
    target = me * nblk + pos
    origin = select(parent_row[None, :] == target[:, None], d_row * nblk + rank1)
    coarse_new = pick(stage, origin).reshape(1, nblk, restricted.shape[1])
    return (state, coarse_new)


def solution(mesh):
    return jax.shard_map(
        shards,
        mesh=mesh,
        in_specs=(
            P(None, "gx", "gy", "gz"),
            P("gx", ("gy", "gz"), None),
            P("gx", None),
            P(None, "gx", "gy", "gz"),
        ),
        out_specs=(P(None, "gx", "gy", "gz"), P("gx", ("gy", "gz"), None)),
        check_vma=False,
    )
```

```python
import jax
import jax.numpy as jnp
from jax import lax
from jax.experimental import pallas as pl
from jax.experimental.pallas import tpu as pltpu
from jax.sharding import PartitionSpec as P

BS = 16

GAMMA = 1.4
LAMBDA = 0.05


def shift_in(plane, axis, forward):
    count = lax.axis_size(axis)
    if forward:
        pairs = [(i, (i + 1) % count) for i in range(count)]
    else:
        pairs = [((i + 1) % count, i) for i in range(count)]
    return lax.ppermute(plane, axis, pairs)


def prims(v):
    rho, mx, my, mz, energy = v
    ux = mx / rho
    uy = my / rho
    uz = mz / rho
    press = (GAMMA - 1.0) * (energy - 0.5 * (mx * ux + my * uy + mz * uz))
    sound = jnp.sqrt(GAMMA * press / rho)
    return (ux, uy, uz), press, sound


def flux_of(v, prim, direc):
    rho, mx, my, mz, energy = v
    vel, press, sound = prim
    normal = vel[direc]
    mom = (mx, my, mz)
    parts = [mom[direc], mx * normal, my * normal, mz * normal, (energy + press) * normal]
    parts[1 + direc] = parts[1 + direc] + press
    return parts, jnp.abs(normal) + sound


def face_of(fa, sa, va, fb, sb, vb):
    wave = 0.5 * jnp.maximum(sa, sb)
    return [0.5 * (fa[i] + fb[i]) - wave * (vb[i] - va[i]) for i in range(5)]


def substep_kernel(u_ref, gx_ref, gy_ref, zfix_ref, zflag_ref, o_ref):
    nx = u_ref.shape[1]
    ny = u_ref.shape[2]
    nz = u_ref.shape[3]
    row = lax.broadcasted_iota(jnp.int32, (ny, nz), 0)
    over_lo = zflag_ref[0] != 0
    over_hi = zflag_ref[1] != 0

    def body(x, carry):
        cen = [u_ref[f, x] for f in range(5)]
        below = jnp.maximum(x - 1, 0)
        above = jnp.minimum(x + 1, nx - 1)
        xm = [jnp.where(x == 0, gx_ref[0, f], u_ref[f, below]) for f in range(5)]
        xp = [jnp.where(x == nx - 1, gx_ref[1, f], u_ref[f, above]) for f in range(5)]
        ym = [
            jnp.where(row == 0, jnp.broadcast_to(gy_ref[0, x, f], (ny, nz)), pltpu.roll(cen[f], 1, 0))
            for f in range(5)
        ]
        yp = [
            jnp.where(
                row == ny - 1, jnp.broadcast_to(gy_ref[1, x, f], (ny, nz)), pltpu.roll(cen[f], ny - 1, 0)
            )
            for f in range(5)
        ]
        zm = [jnp.where(over_lo, zfix_ref[f, x], pltpu.roll(cen[f], 1, 1)) for f in range(5)]
        zp = [jnp.where(over_hi, zfix_ref[f, x], pltpu.roll(cen[f], nz - 1, 1)) for f in range(5)]
        pc = prims(cen)
        total = None
        for direc, (lo, hi) in enumerate(((xm, xp), (ym, yp), (zm, zp))):
            fc, sc = flux_of(cen, pc, direc)
            fl, sl = flux_of(lo, prims(lo), direc)
            fh, sh = flux_of(hi, prims(hi), direc)
            left = face_of(fl, sl, lo, fc, sc, cen)
            right = face_of(fc, sc, cen, fh, sh, hi)
            diff = [right[i] - left[i] for i in range(5)]
            total = diff if total is None else [total[i] + diff[i] for i in range(5)]
        for f in range(5):
            o_ref[f, x] = cen[f] - LAMBDA * total[f]
        return carry

    lax.fori_loop(0, nx, body, 0)


def substep(state, gx, gy, zfix, zflag):
    return pl.pallas_call(
        substep_kernel, out_shape=jax.ShapeDtypeStruct(state.shape, state.dtype)
    )(state, gx, gy, zfix, zflag)


def replicate(rows, cols):
    step = cols // rows
    return (jnp.arange(cols)[None, :] // step == jnp.arange(rows)[:, None]).astype(jnp.float32)


def exact_dot(spec, *ops):
    return jnp.einsum(spec, *ops, precision=lax.Precision.HIGHEST, preferred_element_type=jnp.float32)


def coarse_faces(fetched, nblk):
    half = BS // 2
    lv = fetched.reshape(nblk, -1, 6, 5, half, half)
    rows = replicate(half, BS)
    side = lv[:, :, 0:4].transpose(1, 2, 3, 4, 0, 5).reshape(lv.shape[1], 4, 5, half, nblk * half)
    side = exact_dot("ay,lkfab,bz->lkfyz", rows, side, replicate(nblk * half, nblk * BS))
    ends = lv[:, :, 4:6].transpose(1, 2, 3, 4, 5, 0)
    ends = exact_dot("ax,by,lkfabc,cz->lkfxyz", rows, rows, ends, replicate(nblk, nblk * BS))
    return side, ends


def ghost_inputs(state, side, ends, links):
    nz_dev = state.shape[3]
    chosen = [jnp.repeat(links[:, face] == 1, BS)[None, None, :] for face in range(4)]
    gx = jnp.stack(
        [
            jnp.where(chosen[0], shift_in(state[:, -1], "gx", True), side[0]),
            jnp.where(chosen[1], shift_in(state[:, 0], "gx", False), side[1]),
        ]
    )
    gy = jnp.stack(
        [
            jnp.where(chosen[2], shift_in(state[:, :, -1], "gy", True), side[2]),
            jnp.where(chosen[3], shift_in(state[:, :, 0], "gy", False), side[3]),
        ]
    )
    gy = gy.transpose(0, 2, 1, 3)[:, :, :, None, :]
    far_lo = shift_in(state[..., -1], "gz", True)
    far_hi = shift_in(state[..., 0], "gz", False)
    lane = jnp.arange(nz_dev, dtype=jnp.int32)
    at_lo = lane % BS == 0
    at_hi = lane % BS == BS - 1
    link_lo = jnp.repeat(links[:, 4] == 1, BS)
    link_hi = jnp.repeat(links[:, 5] == 1, BS)
    lo_val = jnp.where(link_lo & (lane == 0), far_lo[..., None], ends[0])
    hi_val = jnp.where(link_hi & (lane == nz_dev - 1), far_hi[..., None], ends[1])
    zfix = jnp.where(at_lo, lo_val, hi_val)
    flag_lo = at_lo & (~link_lo | (lane == 0))
    flag_hi = at_hi & (~link_hi | (lane == nz_dev - 1))
    zflag = jnp.broadcast_to(
        jnp.stack([flag_lo, flag_hi]).astype(jnp.int32)[:, None, :], (2, state.shape[2], nz_dev)
    )
    return gx, gy, zfix, zflag


def restrict_state(state, nblk):
    half = BS // 2
    nz_dev = state.shape[3]
    pairs = state.reshape(5, half, 2, BS, nz_dev)
    planes = pairs[:, :, 0] + pairs[:, :, 1]
    means = 0.125 * exact_dot(
        "ay,fxyl,lm->fxam", replicate(half, BS), planes, replicate(nblk * half, nz_dev).T
    )
    means = means.reshape(5, half, half, nblk, half)
    return means.transpose(3, 0, 1, 2, 4).reshape(nblk, -1)


def pick(table, index):
    flat = table.reshape((-1,) + table.shape[2:])
    return jnp.take(flat, index.reshape(-1), axis=0, mode="clip").reshape(
        index.shape + table.shape[2:]
    )


def select(mask, value):
    return jnp.sum(jnp.where(mask, value, 0), axis=-1)


def shards(fine, shell, parent, link):
    nz_dev = fine.shape[3]
    nblk = nz_dev // BS
    rows = lax.axis_size("gy")
    cols = lax.axis_size("gz")
    my = lax.axis_index("gy")
    mz = lax.axis_index("gz")
    me = my * cols + mz
    parent_row = parent[0]
    count = parent_row.shape[0]
    links = link[:, 0, 0, :].T
    width = shell.shape[2] // 2

    item = jnp.arange(count, dtype=jnp.int32)
    dev = item // nblk
    d_row = dev // cols
    d_col = dev % cols
    owner = parent_row // nblk
    slot = parent_row % nblk
    o_row = owner // cols
    o_col = owner % cols
    before = item[None, :] < item[:, None]
    rank1 = jnp.sum(
        (before & (owner[None, :] == owner[:, None]) & (d_row[None, :] == d_row[:, None])).astype(
            jnp.int32
        ),
        axis=1,
    )
    rank2 = jnp.sum(
        (before & (dev[None, :] == dev[:, None]) & (o_col[None, :] == o_col[:, None])).astype(
            jnp.int32
        ),
        axis=1,
    )
    peer_r = jnp.arange(rows, dtype=jnp.int32)[:, None, None]
    peer_c = jnp.arange(cols, dtype=jnp.int32)[:, None, None]
    cell = jnp.arange(nblk, dtype=jnp.int32)[None, :, None]
    via_me = (d_row == my) & (o_col == mz)

    local = shell[0]
    levels = jnp.concatenate(
        [local[:, :width], 0.5 * (local[:, :width] + local[:, width:])], axis=1
    )
    first = select((owner == me) & (d_row == peer_r) & (rank1 == cell), slot)
    second = select(via_me & (d_col == peer_c) & (rank2 == cell), o_row * nblk + rank1)
    mine = lax.dynamic_slice_in_dim(item, me * nblk, nblk)
    last = o_col[mine] * nblk + rank2[mine]

    def route(rows_of):
        stage = lax.all_to_all(pick(rows_of[None], first), "gy", 0, 0, tiled=True)
        stage = lax.all_to_all(pick(stage, second), "gz", 0, 0, tiled=True)
        return pick(stage, last)

    state = fine
    for step in range(2):
        side, ends = coarse_faces(route(levels[:, step * width : (step + 1) * width]), nblk)
        state = substep(state, *ghost_inputs(state, side[0], ends[0], links))
    restricted = restrict_state(state, nblk)

    pos = jnp.arange(nblk, dtype=jnp.int32)
    back = select(
        (o_col[mine][None, None, :] == peer_c) & (rank2[mine][None, None, :] == cell), pos
    )
    stage = lax.all_to_all(pick(restricted[None], back), "gz", 0, 0, tiled=True)
    home = select(via_me & (o_row == peer_r) & (rank1 == cell), d_col * nblk + rank2)
    stage = lax.all_to_all(pick(stage, home), "gy", 0, 0, tiled=True)
    target = me * nblk + pos
    origin = select(parent_row[None, :] == target[:, None], d_row * nblk + rank1)
    coarse_new = pick(stage, origin).reshape(1, nblk, restricted.shape[1])
    return (state, coarse_new)


def solution(mesh):
    return jax.shard_map(
        shards,
        mesh=mesh,
        in_specs=(
            P(None, "gx", "gy", "gz"),
            P("gx", ("gy", "gz"), None),
            P("gx", None),
            P(None, "gx", "gy", "gz"),
        ),
        out_specs=(P(None, "gx", "gy", "gz"), P("gx", ("gy", "gz"), None)),
        check_vma=False,
    )
```

```python
import jax
import jax.numpy as jnp
from jax import lax
from jax.experimental import pallas as pl
from jax.experimental.pallas import tpu as pltpu
from jax.sharding import PartitionSpec as P

BS = 16

GAMMA = 1.4
LAMBDA = 0.05


def shift_in(plane, axis, forward):
    count = lax.axis_size(axis)
    if forward:
        pairs = [(i, (i + 1) % count) for i in range(count)]
    else:
        pairs = [((i + 1) % count, i) for i in range(count)]
    return lax.ppermute(plane, axis, pairs)


def prims(v):
    rho, mx, my, mz, energy = v
    ux = mx / rho
    uy = my / rho
    uz = mz / rho
    press = (GAMMA - 1.0) * (energy - 0.5 * (mx * ux + my * uy + mz * uz))
    sound = jnp.sqrt(GAMMA * press / rho)
    return (ux, uy, uz), press, sound


def flux_of(v, prim, direc):
    rho, mx, my, mz, energy = v
    vel, press, sound = prim
    normal = vel[direc]
    mom = (mx, my, mz)
    parts = [mom[direc], mx * normal, my * normal, mz * normal, (energy + press) * normal]
    parts[1 + direc] = parts[1 + direc] + press
    return parts, jnp.abs(normal) + sound


def face_of(fa, sa, va, fb, sb, vb):
    wave = 0.5 * jnp.maximum(sa, sb)
    return [0.5 * (fa[i] + fb[i]) - wave * (vb[i] - va[i]) for i in range(5)]


def substep_kernel(u_ref, gx_ref, gy_ref, zfix_ref, zflag_ref, o_ref):
    nx = u_ref.shape[1]
    ny = u_ref.shape[2]
    nz = u_ref.shape[3]
    row = lax.broadcasted_iota(jnp.int32, (ny, nz), 0)
    over_lo = zflag_ref[0] != 0
    over_hi = zflag_ref[1] != 0

    def body(x, carry):
        cen = [u_ref[f, x] for f in range(5)]
        below = jnp.maximum(x - 1, 0)
        above = jnp.minimum(x + 1, nx - 1)
        xm = [jnp.where(x == 0, gx_ref[0, f], u_ref[f, below]) for f in range(5)]
        xp = [jnp.where(x == nx - 1, gx_ref[1, f], u_ref[f, above]) for f in range(5)]
        ym = [
            jnp.where(row == 0, jnp.broadcast_to(gy_ref[0, x, f], (ny, nz)), pltpu.roll(cen[f], 1, 0))
            for f in range(5)
        ]
        yp = [
            jnp.where(
                row == ny - 1, jnp.broadcast_to(gy_ref[1, x, f], (ny, nz)), pltpu.roll(cen[f], ny - 1, 0)
            )
            for f in range(5)
        ]
        zm = [jnp.where(over_lo, zfix_ref[f, x], pltpu.roll(cen[f], 1, 1)) for f in range(5)]
        zp = [jnp.where(over_hi, zfix_ref[f, x], pltpu.roll(cen[f], nz - 1, 1)) for f in range(5)]
        pc = prims(cen)
        total = None
        for direc, (lo, hi) in enumerate(((xm, xp), (ym, yp), (zm, zp))):
            fc, sc = flux_of(cen, pc, direc)
            fl, sl = flux_of(lo, prims(lo), direc)
            fh, sh = flux_of(hi, prims(hi), direc)
            left = face_of(fl, sl, lo, fc, sc, cen)
            right = face_of(fc, sc, cen, fh, sh, hi)
            diff = [right[i] - left[i] for i in range(5)]
            total = diff if total is None else [total[i] + diff[i] for i in range(5)]
        for f in range(5):
            o_ref[f, x] = cen[f] - LAMBDA * total[f]
        return carry

    lax.fori_loop(0, nx, body, 0)


def substep(state, gx, gy, zfix, zflag):
    return pl.pallas_call(
        substep_kernel, out_shape=jax.ShapeDtypeStruct(state.shape, state.dtype)
    )(state, gx, gy, zfix, zflag)


def replicate(rows, cols):
    step = cols // rows
    return (jnp.arange(cols)[None, :] // step == jnp.arange(rows)[:, None]).astype(jnp.float32)


def exact_dot(spec, *ops):
    return jnp.einsum(spec, *ops, precision=lax.Precision.HIGHEST, preferred_element_type=jnp.float32)


def coarse_faces(fetched, nblk):
    half = BS // 2
    lv = fetched.reshape(nblk, 2, 6, 5, half, half)
    rows = replicate(half, BS)
    side = lv[:, :, 0:4].transpose(1, 2, 3, 4, 0, 5).reshape(2, 4, 5, half, nblk * half)
    side = exact_dot("ay,lkfab,bz->lkfyz", rows, side, replicate(nblk * half, nblk * BS))
    ends = lv[:, :, 4:6].transpose(1, 2, 3, 4, 5, 0)
    lane = jnp.arange(nblk * BS)
    starts = (lane % BS == 0)[None, :]
    spread = replicate(nblk, nblk * BS)
    choose = jnp.stack([jnp.where(starts, spread, 0.0), jnp.where(starts, 0.0, spread)])
    ends = exact_dot("ax,by,lkfabc,kcz->lfxyz", rows, rows, ends, choose)
    return side, ends


def ghost_inputs(state, side, ends, links):
    nz_dev = state.shape[3]
    chosen = [jnp.repeat(links[:, face] == 1, BS)[None, None, :] for face in range(4)]
    gx = jnp.stack(
        [
            jnp.where(chosen[0], shift_in(state[:, -1], "gx", True), side[0]),
            jnp.where(chosen[1], shift_in(state[:, 0], "gx", False), side[1]),
        ]
    )
    gy = jnp.stack(
        [
            jnp.where(chosen[2], shift_in(state[:, :, -1], "gy", True), side[2]),
            jnp.where(chosen[3], shift_in(state[:, :, 0], "gy", False), side[3]),
        ]
    )
    gy = gy.transpose(0, 2, 1, 3)[:, :, :, None, :]
    far_lo = shift_in(state[..., -1], "gz", True)
    far_hi = shift_in(state[..., 0], "gz", False)
    lane = jnp.arange(nz_dev, dtype=jnp.int32)
    at_lo = lane % BS == 0
    at_hi = lane % BS == BS - 1
    link_lo = jnp.repeat(links[:, 4] == 1, BS)
    link_hi = jnp.repeat(links[:, 5] == 1, BS)
    zfix = jnp.where(
        link_lo & (lane == 0),
        far_lo[..., None],
        jnp.where(link_hi & (lane == nz_dev - 1), far_hi[..., None], ends),
    )
    flag_lo = at_lo & (~link_lo | (lane == 0))
    flag_hi = at_hi & (~link_hi | (lane == nz_dev - 1))
    zflag = jnp.broadcast_to(
        jnp.stack([flag_lo, flag_hi]).astype(jnp.int32)[:, None, :], (2, state.shape[2], nz_dev)
    )
    return gx, gy, zfix, zflag


def restrict_state(state, nblk):
    half = BS // 2
    nz_dev = state.shape[3]
    pairs = state.reshape(5, half, 2, BS, nz_dev)
    planes = pairs[:, :, 0] + pairs[:, :, 1]
    means = 0.125 * exact_dot(
        "ay,fxyl,lm->fxam", replicate(half, BS), planes, replicate(nblk * half, nz_dev).T
    )
    means = means.reshape(5, half, half, nblk, half)
    return means.transpose(3, 0, 1, 2, 4).reshape(nblk, -1)


def pick(table, index):
    flat = table.reshape((-1,) + table.shape[2:])
    return jnp.take(flat, index.reshape(-1), axis=0, mode="clip").reshape(
        index.shape + table.shape[2:]
    )


def select(mask, value):
    return jnp.sum(jnp.where(mask, value, 0), axis=-1)


def shards(fine, shell, parent, link):
    nz_dev = fine.shape[3]
    nblk = nz_dev // BS
    rows = lax.axis_size("gy")
    cols = lax.axis_size("gz")
    my = lax.axis_index("gy")
    mz = lax.axis_index("gz")
    me = my * cols + mz
    parent_row = parent[0]
    count = parent_row.shape[0]
    links = link[:, 0, 0, :].T
    width = shell.shape[2] // 2

    item = jnp.arange(count, dtype=jnp.int32)
    dev = item // nblk
    d_row = dev // cols
    d_col = dev % cols
    owner = parent_row // nblk
    slot = parent_row % nblk
    o_row = owner // cols
    o_col = owner % cols
    before = item[None, :] < item[:, None]
    rank1 = jnp.sum(
        (before & (owner[None, :] == owner[:, None]) & (d_row[None, :] == d_row[:, None])).astype(
            jnp.int32
        ),
        axis=1,
    )
    rank2 = jnp.sum(
        (before & (dev[None, :] == dev[:, None]) & (o_col[None, :] == o_col[:, None])).astype(
            jnp.int32
        ),
        axis=1,
    )
    peer_r = jnp.arange(rows, dtype=jnp.int32)[:, None, None]
    peer_c = jnp.arange(cols, dtype=jnp.int32)[:, None, None]
    cell = jnp.arange(nblk, dtype=jnp.int32)[None, :, None]
    via_me = (d_row == my) & (o_col == mz)

    local = shell[0]
    levels = jnp.concatenate(
        [local[:, :width], 0.5 * (local[:, :width] + local[:, width:])], axis=1
    )
    first = select((owner == me) & (d_row == peer_r) & (rank1 == cell), slot)
    stage = lax.all_to_all(pick(levels[None], first), "gy", 0, 0, tiled=True)
    second = select(via_me & (d_col == peer_c) & (rank2 == cell), o_row * nblk + rank1)
    stage = lax.all_to_all(pick(stage, second), "gz", 0, 0, tiled=True)
    mine = lax.dynamic_slice_in_dim(item, me * nblk, nblk)
    fetched = pick(stage, o_col[mine] * nblk + rank2[mine])

    side, ends = coarse_faces(fetched, nblk)
    state = fine
    for step in range(2):
        state = substep(state, *ghost_inputs(state, side[step], ends[step], links))
    restricted = restrict_state(state, nblk)

    pos = jnp.arange(nblk, dtype=jnp.int32)
    back = select(
        (o_col[mine][None, None, :] == peer_c) & (rank2[mine][None, None, :] == cell), pos
    )
    stage = lax.all_to_all(pick(restricted[None], back), "gz", 0, 0, tiled=True)
    home = select(via_me & (o_row == peer_r) & (rank1 == cell), d_col * nblk + rank2)
    stage = lax.all_to_all(pick(stage, home), "gy", 0, 0, tiled=True)
    target = me * nblk + pos
    origin = select(parent_row[None, :] == target[:, None], d_row * nblk + rank1)
    coarse_new = pick(stage, origin).reshape(1, nblk, restricted.shape[1])
    return (state, coarse_new)


def solution(mesh):
    return jax.shard_map(
        shards,
        mesh=mesh,
        in_specs=(
            P(None, "gx", "gy", "gz"),
            P("gx", ("gy", "gz"), None),
            P("gx", None),
            P(None, "gx", "gy", "gz"),
        ),
        out_specs=(P(None, "gx", "gy", "gz"), P("gx", ("gy", "gz"), None)),
        check_vma=False,
    )
```

```python
import jax
import jax.numpy as jnp
from jax import lax
from jax.experimental import pallas as pl
from jax.experimental.pallas import tpu as pltpu
from jax.sharding import PartitionSpec as P

BS = 16

GAMMA = 1.4
LAMBDA = 0.05


def shift_in(plane, axis, forward):
    count = lax.axis_size(axis)
    if forward:
        pairs = [(i, (i + 1) % count) for i in range(count)]
    else:
        pairs = [((i + 1) % count, i) for i in range(count)]
    return lax.ppermute(plane, axis, pairs)


def prims(v):
    rho, mx, my, mz, energy = v
    ux = mx / rho
    uy = my / rho
    uz = mz / rho
    press = (GAMMA - 1.0) * (energy - 0.5 * (mx * ux + my * uy + mz * uz))
    sound = jnp.sqrt(GAMMA * press / rho)
    return (ux, uy, uz), press, sound


def flux_of(v, prim, direc):
    rho, mx, my, mz, energy = v
    vel, press, sound = prim
    normal = vel[direc]
    mom = (mx, my, mz)
    parts = [mom[direc], mx * normal, my * normal, mz * normal, (energy + press) * normal]
    parts[1 + direc] = parts[1 + direc] + press
    return parts, jnp.abs(normal) + sound


def face_of(fa, sa, va, fb, sb, vb):
    wave = 0.5 * jnp.maximum(sa, sb)
    return [0.5 * (fa[i] + fb[i]) - wave * (vb[i] - va[i]) for i in range(5)]


def substep_kernel(u_ref, gx_ref, gy_ref, zfix_ref, zflag_ref, o_ref, ox_ref, oy_ref, oz_ref):
    nx = u_ref.shape[1]
    ny = u_ref.shape[2]
    nz = u_ref.shape[3]
    row = lax.broadcasted_iota(jnp.int32, (ny, nz), 0)
    over_lo = zflag_ref[0] != 0
    over_hi = zflag_ref[1] != 0

    def body(x, carry):
        cen = [u_ref[f, x] for f in range(5)]
        below = jnp.maximum(x - 1, 0)
        above = jnp.minimum(x + 1, nx - 1)
        xm = [jnp.where(x == 0, gx_ref[0, f], u_ref[f, below]) for f in range(5)]
        xp = [jnp.where(x == nx - 1, gx_ref[1, f], u_ref[f, above]) for f in range(5)]
        ym = [
            jnp.where(row == 0, jnp.broadcast_to(gy_ref[0, x, f], (ny, nz)), pltpu.roll(cen[f], 1, 0))
            for f in range(5)
        ]
        yp = [
            jnp.where(
                row == ny - 1, jnp.broadcast_to(gy_ref[1, x, f], (ny, nz)), pltpu.roll(cen[f], ny - 1, 0)
            )
            for f in range(5)
        ]
        zm = [jnp.where(over_lo, zfix_ref[f, x], pltpu.roll(cen[f], 1, 1)) for f in range(5)]
        zp = [jnp.where(over_hi, zfix_ref[f, x], pltpu.roll(cen[f], nz - 1, 1)) for f in range(5)]
        pc = prims(cen)
        total = None
        for direc, (lo, hi) in enumerate(((xm, xp), (ym, yp), (zm, zp))):
            fc, sc = flux_of(cen, pc, direc)
            fl, sl = flux_of(lo, prims(lo), direc)
            fh, sh = flux_of(hi, prims(hi), direc)
            left = face_of(fl, sl, lo, fc, sc, cen)
            right = face_of(fc, sc, cen, fh, sh, hi)
            diff = [right[i] - left[i] for i in range(5)]
            total = diff if total is None else [total[i] + diff[i] for i in range(5)]
        new = [cen[f] - LAMBDA * total[f] for f in range(5)]
        for f in range(5):
            o_ref[f, x] = new[f]
            oy_ref[0, x, f] = new[f][ny - 1 : ny, :]
            oy_ref[1, x, f] = new[f][0:1, :]
            oz_ref[0, f, x] = new[f][:, nz - 1 : nz]
            oz_ref[1, f, x] = new[f][:, 0:1]

        @pl.when(x == nx - 1)
        def _():
            for f in range(5):
                ox_ref[0, f] = new[f]

        @pl.when(x == 0)
        def _():
            for f in range(5):
                ox_ref[1, f] = new[f]

        return carry

    lax.fori_loop(0, nx, body, 0)


def substep(state, gx, gy, zfix, zflag):
    five, nx, ny, nz = state.shape
    shapes = [state.shape, (2, five, ny, nz), (2, nx, five, 1, nz), (2, five, nx, ny, 1)]
    out = pl.pallas_call(
        substep_kernel, out_shape=[jax.ShapeDtypeStruct(one, state.dtype) for one in shapes]
    )(state, gx, gy, zfix, zflag)
    return out[0], out[1:]


def planes_of(state):
    ox = jnp.stack([state[:, -1], state[:, 0]])
    oy = jnp.stack([state[:, :, -1], state[:, :, 0]]).transpose(0, 2, 1, 3)[:, :, :, None, :]
    oz = jnp.stack([state[..., -1], state[..., 0]])[..., None]
    return ox, oy, oz


def replicate(rows, cols):
    step = cols // rows
    return (jnp.arange(cols)[None, :] // step == jnp.arange(rows)[:, None]).astype(jnp.float32)


def exact_dot(spec, *ops):
    return jnp.einsum(spec, *ops, precision=lax.Precision.HIGHEST, preferred_element_type=jnp.float32)


def coarse_faces(fetched, nblk):
    half = BS // 2
    lv = fetched.reshape(nblk, 2, 6, 5, half, half)
    rows = replicate(half, BS)
    side = lv[:, :, 0:4].transpose(1, 2, 3, 4, 0, 5).reshape(2, 4, 5, half, nblk * half)
    side = exact_dot("ay,lkfab,bz->lkfyz", rows, side, replicate(nblk * half, nblk * BS))
    ends = lv[:, :, 4:6].transpose(1, 2, 3, 4, 5, 0)
    lane = jnp.arange(nblk * BS)
    starts = (lane % BS == 0)[None, :]
    spread = replicate(nblk, nblk * BS)
    choose = jnp.stack([jnp.where(starts, spread, 0.0), jnp.where(starts, 0.0, spread)])
    ends = exact_dot("ax,by,lkfabc,kcz->lfxyz", rows, rows, ends, choose)
    return side, ends


def ghost_inputs(state, planes, side, ends, links):
    nz_dev = state.shape[3]
    ox, oy, oz = planes
    chosen = [jnp.repeat(links[:, face] == 1, BS)[None, None, :] for face in range(4)]
    gx = jnp.stack(
        [
            jnp.where(chosen[0], shift_in(ox[0], "gx", True), side[0]),
            jnp.where(chosen[1], shift_in(ox[1], "gx", False), side[1]),
        ]
    )
    gy = jnp.stack(
        [
            jnp.where(chosen[2], shift_in(oy[0], "gy", True), side[2]),
            jnp.where(chosen[3], shift_in(oy[1], "gy", False), side[3]),
        ]
    )
    far_lo = shift_in(oz[0], "gz", True)
    far_hi = shift_in(oz[1], "gz", False)
    lane = jnp.arange(nz_dev, dtype=jnp.int32)
    at_lo = lane % BS == 0
    at_hi = lane % BS == BS - 1
    link_lo = jnp.repeat(links[:, 4] == 1, BS)
    link_hi = jnp.repeat(links[:, 5] == 1, BS)
    zfix = jnp.where(
        link_lo & (lane == 0),
        far_lo,
        jnp.where(link_hi & (lane == nz_dev - 1), far_hi, ends),
    )
    flag_lo = at_lo & (~link_lo | (lane == 0))
    flag_hi = at_hi & (~link_hi | (lane == nz_dev - 1))
    zflag = jnp.broadcast_to(
        jnp.stack([flag_lo, flag_hi]).astype(jnp.int32)[:, None, :], (2, state.shape[2], nz_dev)
    )
    return gx, gy, zfix, zflag


def restrict_state(state, nblk):
    half = BS // 2
    nz_dev = state.shape[3]
    pairs = state.reshape(5, half, 2, BS, nz_dev)
    planes = pairs[:, :, 0] + pairs[:, :, 1]
    means = 0.125 * exact_dot(
        "ay,fxyl,lm->fxam", replicate(half, BS), planes, replicate(nblk * half, nz_dev).T
    )
    means = means.reshape(5, half, half, nblk, half)
    return means.transpose(3, 0, 1, 2, 4).reshape(nblk, -1)


def pick(table, index):
    flat = table.reshape((-1,) + table.shape[2:])
    return jnp.take(flat, index.reshape(-1), axis=0, mode="clip").reshape(
        index.shape + table.shape[2:]
    )


def select(mask, value):
    return jnp.sum(jnp.where(mask, value, 0), axis=-1)


def shards(fine, shell, parent, link):
    nz_dev = fine.shape[3]
    nblk = nz_dev // BS
    rows = lax.axis_size("gy")
    cols = lax.axis_size("gz")
    my = lax.axis_index("gy")
    mz = lax.axis_index("gz")
    me = my * cols + mz
    parent_row = parent[0]
    count = parent_row.shape[0]
    links = link[:, 0, 0, :].T
    width = shell.shape[2] // 2

    item = jnp.arange(count, dtype=jnp.int32)
    dev = item // nblk
    d_row = dev // cols
    d_col = dev % cols
    owner = parent_row // nblk
    slot = parent_row % nblk
    o_row = owner // cols
    o_col = owner % cols
    before = item[None, :] < item[:, None]
    rank1 = jnp.sum(
        (before & (owner[None, :] == owner[:, None]) & (d_row[None, :] == d_row[:, None])).astype(
            jnp.int32
        ),
        axis=1,
    )
    rank2 = jnp.sum(
        (before & (dev[None, :] == dev[:, None]) & (o_col[None, :] == o_col[:, None])).astype(
            jnp.int32
        ),
        axis=1,
    )
    peer_r = jnp.arange(rows, dtype=jnp.int32)[:, None, None]
    peer_c = jnp.arange(cols, dtype=jnp.int32)[:, None, None]
    cell = jnp.arange(nblk, dtype=jnp.int32)[None, :, None]
    via_me = (d_row == my) & (o_col == mz)

    local = shell[0]
    levels = jnp.concatenate(
        [local[:, :width], 0.5 * (local[:, :width] + local[:, width:])], axis=1
    )
    first = select((owner == me) & (d_row == peer_r) & (rank1 == cell), slot)
    stage = lax.all_to_all(pick(levels[None], first), "gy", 0, 0, tiled=True)
    second = select(via_me & (d_col == peer_c) & (rank2 == cell), o_row * nblk + rank1)
    stage = lax.all_to_all(pick(stage, second), "gz", 0, 0, tiled=True)
    mine = lax.dynamic_slice_in_dim(item, me * nblk, nblk)
    fetched = pick(stage, o_col[mine] * nblk + rank2[mine])

    side, ends = coarse_faces(fetched, nblk)
    side = [side[:, 0], side[:, 1], side[:, 2].transpose(0, 2, 1, 3)[:, :, :, None, :],
            side[:, 3].transpose(0, 2, 1, 3)[:, :, :, None, :]]
    state = fine
    planes = planes_of(fine)
    for step in range(2):
        level_side = [one[step] for one in side]
        state, planes = substep(state, *ghost_inputs(state, planes, level_side, ends[step], links))
    restricted = restrict_state(state, nblk)

    pos = jnp.arange(nblk, dtype=jnp.int32)
    back = select(
        (o_col[mine][None, None, :] == peer_c) & (rank2[mine][None, None, :] == cell), pos
    )
    stage = lax.all_to_all(pick(restricted[None], back), "gz", 0, 0, tiled=True)
    home = select(via_me & (o_row == peer_r) & (rank1 == cell), d_col * nblk + rank2)
    stage = lax.all_to_all(pick(stage, home), "gy", 0, 0, tiled=True)
    target = me * nblk + pos
    origin = select(parent_row[None, :] == target[:, None], d_row * nblk + rank1)
    coarse_new = pick(stage, origin).reshape(1, nblk, restricted.shape[1])
    return (state, coarse_new)


def solution(mesh):
    return jax.shard_map(
        shards,
        mesh=mesh,
        in_specs=(
            P(None, "gx", "gy", "gz"),
            P("gx", ("gy", "gz"), None),
            P("gx", None),
            P(None, "gx", "gy", "gz"),
        ),
        out_specs=(P(None, "gx", "gy", "gz"), P("gx", ("gy", "gz"), None)),
        check_vma=False,
    )
```

```python
import jax
import jax.numpy as jnp
from jax import lax
from jax.experimental import pallas as pl
from jax.experimental.pallas import tpu as pltpu
from jax.sharding import PartitionSpec as P

BS = 16

GAMMA = 1.4
LAMBDA = 0.05


def shift_in(plane, axis, forward):
    count = lax.axis_size(axis)
    if forward:
        pairs = [(i, (i + 1) % count) for i in range(count)]
    else:
        pairs = [((i + 1) % count, i) for i in range(count)]
    return lax.ppermute(plane, axis, pairs)


def prims(v):
    rho, mx, my, mz, energy = v
    ux = mx / rho
    uy = my / rho
    uz = mz / rho
    press = (GAMMA - 1.0) * (energy - 0.5 * (mx * ux + my * uy + mz * uz))
    sound = jnp.sqrt(GAMMA * press / rho)
    return (ux, uy, uz), press, sound


def flux_of(v, prim, direc):
    _, mx, my, mz, energy = v
    vel, press, sound = prim
    normal = vel[direc]
    mom = (mx, my, mz)
    parts = [mom[direc], mx * normal, my * normal, mz * normal, (energy + press) * normal]
    parts[1 + direc] = parts[1 + direc] + press
    return parts, jnp.abs(normal) + sound


def face_of(fa, sa, va, fb, sb, vb):
    wave = 0.5 * jnp.maximum(sa, sb)
    return [0.5 * (fa[i] + fb[i]) - wave * (vb[i] - va[i]) for i in range(5)]


def substep_kernel(u_ref, gx_ref, gy_ref, zfix_ref, zflag_ref, o_ref):
    nx = u_ref.shape[1]
    ny = u_ref.shape[2]
    nz = u_ref.shape[3]
    row = lax.broadcasted_iota(jnp.int32, (ny, nz), 0)
    over_lo = zflag_ref[0] != 0
    over_hi = zflag_ref[1] != 0

    def body(x, carry):
        cen = [u_ref[f, x] for f in range(5)]
        below = jnp.maximum(x - 1, 0)
        above = jnp.minimum(x + 1, nx - 1)
        xm = [jnp.where(x == 0, gx_ref[0, f], u_ref[f, below]) for f in range(5)]
        xp = [jnp.where(x == nx - 1, gx_ref[1, f], u_ref[f, above]) for f in range(5)]
        ym = [
            jnp.where(row == 0, jnp.broadcast_to(gy_ref[0, x, f], (ny, nz)), pltpu.roll(cen[f], 1, 0))
            for f in range(5)
        ]
        yp = [
            jnp.where(
                row == ny - 1, jnp.broadcast_to(gy_ref[1, x, f], (ny, nz)), pltpu.roll(cen[f], ny - 1, 0)
            )
            for f in range(5)
        ]
        zm = [jnp.where(over_lo, zfix_ref[f, x], pltpu.roll(cen[f], 1, 1)) for f in range(5)]
        zp = [jnp.where(over_hi, zfix_ref[f, x], pltpu.roll(cen[f], nz - 1, 1)) for f in range(5)]
        pc = prims(cen)
        total = None
        for direc, (lo, hi) in enumerate(((xm, xp), (ym, yp), (zm, zp))):
            fc, sc = flux_of(cen, pc, direc)
            fl, sl = flux_of(lo, prims(lo), direc)
            fh, sh = flux_of(hi, prims(hi), direc)
            left = face_of(fl, sl, lo, fc, sc, cen)
            right = face_of(fc, sc, cen, fh, sh, hi)
            diff = [right[i] - left[i] for i in range(5)]
            total = diff if total is None else [total[i] + diff[i] for i in range(5)]
        for f in range(5):
            o_ref[f, x] = cen[f] - LAMBDA * total[f]
        return carry

    lax.fori_loop(0, nx, body, 0)


def substep(state, gx, gy, zfix, zflag):
    return pl.pallas_call(
        substep_kernel, out_shape=jax.ShapeDtypeStruct(state.shape, state.dtype)
    )(state, gx, gy, zfix, zflag)


def replicate(rows, cols):
    step = cols // rows
    return (jnp.arange(cols)[None, :] // step == jnp.arange(rows)[:, None]).astype(jnp.float32)


def exact_dot(spec, *ops):
    return jnp.einsum(spec, *ops, precision=lax.Precision.HIGHEST, preferred_element_type=jnp.float32)


def coarse_faces(fetched, nblk):
    half = BS // 2
    lv = fetched.reshape(nblk, 2, 6, 5, half, half)
    rows = replicate(half, BS)
    side = lv[:, :, 0:4].transpose(1, 2, 3, 4, 0, 5).reshape(2, 4, 5, half, nblk * half)
    side = exact_dot("ay,lkfab,bz->lkfyz", rows, side, replicate(nblk * half, nblk * BS))
    ends = lv[:, :, 4:6].transpose(1, 2, 3, 4, 5, 0)
    lane = jnp.arange(nblk * BS)
    starts = (lane % BS == 0)[None, :]
    spread = replicate(nblk, nblk * BS)
    choose = jnp.stack([jnp.where(starts, spread, 0.0), jnp.where(starts, 0.0, spread)])
    ends = exact_dot("ax,by,lkfabc,kcz->lfxyz", rows, rows, ends, choose)
    return side, ends


def ghost_inputs(state, side, ends, links):
    chosen = [jnp.repeat(links[:, face] == 1, BS)[None, None, :] for face in range(4)]
    far_lo = shift_in(state[..., -1], "gz", True)
    far_hi = shift_in(state[..., 0], "gz", False)
    gx, gy = xy_ghosts(state, side, chosen)
    return finish_ghosts(state, gx, gy, far_lo, far_hi, ends, links)


def xy_ghosts(state, side, chosen):
    gx = jnp.stack(
        [
            jnp.where(chosen[0], shift_in(state[:, -1], "gx", True), side[0]),
            jnp.where(chosen[1], shift_in(state[:, 0], "gx", False), side[1]),
        ]
    )
    gy = jnp.stack(
        [
            jnp.where(chosen[2], shift_in(state[:, :, -1], "gy", True), side[2]),
            jnp.where(chosen[3], shift_in(state[:, :, 0], "gy", False), side[3]),
        ]
    )
    return gx, gy.transpose(0, 2, 1, 3)[:, :, :, None, :]


def finish_ghosts(state, gx, gy, far_lo, far_hi, ends, links):
    nz_dev = state.shape[3]
    lane = jnp.arange(nz_dev, dtype=jnp.int32)
    at_lo = lane % BS == 0
    at_hi = lane % BS == BS - 1
    link_lo = jnp.repeat(links[:, 4] == 1, BS)
    link_hi = jnp.repeat(links[:, 5] == 1, BS)
    zfix = jnp.where(
        link_lo & (lane == 0),
        far_lo[..., None],
        jnp.where(link_hi & (lane == nz_dev - 1), far_hi[..., None], ends),
    )
    flag_lo = at_lo & (~link_lo | (lane == 0))
    flag_hi = at_hi & (~link_hi | (lane == nz_dev - 1))
    zflag = jnp.broadcast_to(
        jnp.stack([flag_lo, flag_hi]).astype(jnp.int32)[:, None, :], (2, state.shape[2], nz_dev)
    )
    return gx, gy, zfix, zflag


def restrict_state(state, nblk):
    half = BS // 2
    nz_dev = state.shape[3]
    pairs = state.reshape(5, half, 2, BS, nz_dev)
    planes = pairs[:, :, 0] + pairs[:, :, 1]
    means = 0.125 * exact_dot(
        "ay,fxyl,lm->fxam", replicate(half, BS), planes, replicate(nblk * half, nz_dev).T
    )
    means = means.reshape(5, half, half, nblk, half)
    return means.transpose(3, 0, 1, 2, 4).reshape(nblk, -1)


def pick(table, index):
    flat = table.reshape((-1,) + table.shape[2:])
    return jnp.take(flat, index.reshape(-1), axis=0, mode="clip").reshape(
        index.shape + table.shape[2:]
    )


def select(mask, value):
    return jnp.sum(jnp.where(mask, value, 0), axis=-1)


def shards(fine, shell, parent, link):
    nz_dev = fine.shape[3]
    nblk = nz_dev // BS
    rows = lax.axis_size("gy")
    cols = lax.axis_size("gz")
    my = lax.axis_index("gy")
    mz = lax.axis_index("gz")
    me = my * cols + mz
    parent_row = parent[0]
    count = parent_row.shape[0]
    links = link[:, 0, 0, :].T
    width = shell.shape[2] // 2

    item = jnp.arange(count, dtype=jnp.int32)
    dev = item // nblk
    d_row = dev // cols
    d_col = dev % cols
    owner = parent_row // nblk
    slot = parent_row % nblk
    o_row = owner // cols
    o_col = owner % cols
    before = item[None, :] < item[:, None]
    rank1 = jnp.sum(
        (before & (owner[None, :] == owner[:, None]) & (d_row[None, :] == d_row[:, None])).astype(
            jnp.int32
        ),
        axis=1,
    )
    rank2 = jnp.sum(
        (before & (dev[None, :] == dev[:, None]) & (o_col[None, :] == o_col[:, None])).astype(
            jnp.int32
        ),
        axis=1,
    )
    peer_r = jnp.arange(rows, dtype=jnp.int32)[:, None, None]
    peer_c = jnp.arange(cols, dtype=jnp.int32)[:, None, None]
    cell = jnp.arange(nblk, dtype=jnp.int32)[None, :, None]
    via_me = (d_row == my) & (o_col == mz)

    local = shell[0]
    levels = jnp.concatenate(
        [local[:, :width], 0.5 * (local[:, :width] + local[:, width:])], axis=1
    )
    first = select((owner == me) & (d_row == peer_r) & (rank1 == cell), slot)
    stage = lax.all_to_all(pick(levels[None], first), "gy", 0, 0, tiled=True)
    second = select(via_me & (d_col == peer_c) & (rank2 == cell), o_row * nblk + rank1)
    stage = lax.all_to_all(pick(stage, second), "gz", 0, 0, tiled=True)
    mine = lax.dynamic_slice_in_dim(item, me * nblk, nblk)
    fetched = pick(stage, o_col[mine] * nblk + rank2[mine])

    side, ends = coarse_faces(fetched, nblk)
    state = fine
    for step in range(2):
        state = substep(state, *ghost_inputs(state, side[step], ends[step], links))
    restricted = restrict_state(state, nblk)

    pos = jnp.arange(nblk, dtype=jnp.int32)
    back = select(
        (o_col[mine][None, None, :] == peer_c) & (rank2[mine][None, None, :] == cell), pos
    )
    stage = lax.all_to_all(pick(restricted[None], back), "gz", 0, 0, tiled=True)
    home = select(via_me & (o_row == peer_r) & (rank1 == cell), d_col * nblk + rank2)
    stage = lax.all_to_all(pick(stage, home), "gy", 0, 0, tiled=True)
    target = me * nblk + pos
    origin = select(parent_row[None, :] == target[:, None], d_row * nblk + rank1)
    coarse_new = pick(stage, origin).reshape(1, nblk, restricted.shape[1])
    return (state, coarse_new)


def solution(mesh):
    return step_of(mesh)


def step_of(mesh):
    return jax.shard_map(
        shards,
        mesh=mesh,
        in_specs=(
            P(None, "gx", "gy", "gz"),
            P("gx", ("gy", "gz"), None),
            P("gx", None),
            P(None, "gx", "gy", "gz"),
        ),
        out_specs=(P(None, "gx", "gy", "gz"), P("gx", ("gy", "gz"), None)),
        check_vma=False,
    )
```

```python
import jax
import jax.numpy as jnp
from jax import lax
from jax.experimental import pallas as pl
from jax.experimental.pallas import tpu as pltpu
from jax.sharding import PartitionSpec as P

BS = 16

GAMMA = 1.4
LAMBDA = 0.05


def shift_in(plane, axis, forward):
    count = lax.axis_size(axis)
    if forward:
        pairs = [(i, (i + 1) % count) for i in range(count)]
    else:
        pairs = [((i + 1) % count, i) for i in range(count)]
    return lax.ppermute(plane, axis, pairs)


def prims(v):
    rho, mx, my, mz, energy = v
    ux = mx / rho
    uy = my / rho
    uz = mz / rho
    press = (GAMMA - 1.0) * (energy - 0.5 * (mx * ux + my * uy + mz * uz))
    sound = jnp.sqrt(GAMMA * press / rho)
    return (ux, uy, uz), press, sound


def flux_of(v, prim, direc):
    rho, mx, my, mz, energy = v
    vel, press, sound = prim
    normal = vel[direc]
    mom = (mx, my, mz)
    parts = [mom[direc], mx * normal, my * normal, mz * normal, (energy + press) * normal]
    parts[1 + direc] = parts[1 + direc] + press
    return parts, jnp.abs(normal) + sound


def face_of(fa, sa, va, fb, sb, vb):
    wave = 0.5 * jnp.maximum(sa, sb)
    return [0.5 * (fa[i] + fb[i]) - wave * (vb[i] - va[i]) for i in range(5)]


def substep_kernel(u_ref, gx_ref, gy_ref, zfix_ref, zflag_ref, o_ref):
    nx = u_ref.shape[1]
    ny = u_ref.shape[2]
    nz = u_ref.shape[3]
    row = lax.broadcasted_iota(jnp.int32, (ny, nz), 0)
    over_lo = zflag_ref[0] != 0
    over_hi = zflag_ref[1] != 0

    def body(x, carry):
        cen = [u_ref[f, x] for f in range(5)]
        below = jnp.maximum(x - 1, 0)
        above = jnp.minimum(x + 1, nx - 1)
        xm = [jnp.where(x == 0, gx_ref[0, f], u_ref[f, below]) for f in range(5)]
        xp = [jnp.where(x == nx - 1, gx_ref[1, f], u_ref[f, above]) for f in range(5)]
        ym = [
            jnp.where(row == 0, jnp.broadcast_to(gy_ref[0, x, f], (ny, nz)), pltpu.roll(cen[f], 1, 0))
            for f in range(5)
        ]
        yp = [
            jnp.where(
                row == ny - 1, jnp.broadcast_to(gy_ref[1, x, f], (ny, nz)), pltpu.roll(cen[f], ny - 1, 0)
            )
            for f in range(5)
        ]
        zm = [jnp.where(over_lo, zfix_ref[f, x], pltpu.roll(cen[f], 1, 1)) for f in range(5)]
        zp = [jnp.where(over_hi, zfix_ref[f, x], pltpu.roll(cen[f], nz - 1, 1)) for f in range(5)]
        pc = prims(cen)
        total = None
        for direc, (lo, hi) in enumerate(((xm, xp), (ym, yp), (zm, zp))):
            fc, sc = flux_of(cen, pc, direc)
            fl, sl = flux_of(lo, prims(lo), direc)
            fh, sh = flux_of(hi, prims(hi), direc)
            left = face_of(fl, sl, lo, fc, sc, cen)
            right = face_of(fc, sc, cen, fh, sh, hi)
            diff = [right[i] - left[i] for i in range(5)]
            total = diff if total is None else [total[i] + diff[i] for i in range(5)]
        for f in range(5):
            o_ref[f, x] = cen[f] - LAMBDA * total[f]
        return carry

    lax.fori_loop(0, nx, body, 0)


def substep(state, gx, gy, zfix, zflag):
    return pl.pallas_call(
        substep_kernel, out_shape=jax.ShapeDtypeStruct(state.shape, state.dtype)
    )(state, gx, gy, zfix, zflag)


def replicate(rows, cols):
    step = cols // rows
    return (jnp.arange(cols)[None, :] // step == jnp.arange(rows)[:, None]).astype(jnp.float32)


def exact_dot(spec, *ops):
    return jnp.einsum(spec, *ops, precision=lax.Precision.HIGHEST, preferred_element_type=jnp.float32)


def coarse_faces(fetched, nblk):
    half = BS // 2
    lv = fetched.reshape(nblk, -1, 6, 5, half, half)
    rows = replicate(half, BS)
    side = lv[:, :, 0:4].transpose(1, 2, 3, 4, 0, 5).reshape(lv.shape[1], 4, 5, half, nblk * half)
    side = exact_dot("ay,lkfab,bz->lkfyz", rows, side, replicate(nblk * half, nblk * BS))
    ends = lv[:, :, 4:6].transpose(1, 2, 3, 4, 5, 0)
    lane = jnp.arange(nblk * BS)
    starts = (lane % BS == 0)[None, :]
    spread = replicate(nblk, nblk * BS)
    choose = jnp.stack([jnp.where(starts, spread, 0.0), jnp.where(starts, 0.0, spread)])
    ends = exact_dot("ax,by,lkfabc,kcz->lfxyz", rows, rows, ends, choose)
    return side, ends


def ghost_inputs(state, side, ends, links):
    nz_dev = state.shape[3]
    chosen = [jnp.repeat(links[:, face] == 1, BS)[None, None, :] for face in range(4)]
    gx = jnp.stack(
        [
            jnp.where(chosen[0], shift_in(state[:, -1], "gx", True), side[0]),
            jnp.where(chosen[1], shift_in(state[:, 0], "gx", False), side[1]),
        ]
    )
    gy = jnp.stack(
        [
            jnp.where(chosen[2], shift_in(state[:, :, -1], "gy", True), side[2]),
            jnp.where(chosen[3], shift_in(state[:, :, 0], "gy", False), side[3]),
        ]
    )
    gy = gy.transpose(0, 2, 1, 3)[:, :, :, None, :]
    far_lo = shift_in(state[..., -1], "gz", True)
    far_hi = shift_in(state[..., 0], "gz", False)
    lane = jnp.arange(nz_dev, dtype=jnp.int32)
    at_lo = lane % BS == 0
    at_hi = lane % BS == BS - 1
    link_lo = jnp.repeat(links[:, 4] == 1, BS)
    link_hi = jnp.repeat(links[:, 5] == 1, BS)
    zfix = jnp.where(
        link_lo & (lane == 0),
        far_lo[..., None],
        jnp.where(link_hi & (lane == nz_dev - 1), far_hi[..., None], ends),
    )
    flag_lo = at_lo & (~link_lo | (lane == 0))
    flag_hi = at_hi & (~link_hi | (lane == nz_dev - 1))
    zflag = jnp.broadcast_to(
        jnp.stack([flag_lo, flag_hi]).astype(jnp.int32)[:, None, :], (2, state.shape[2], nz_dev)
    )
    return gx, gy, zfix, zflag


def restrict_state(state, nblk):
    half = BS // 2
    nz_dev = state.shape[3]
    pairs = state.reshape(5, half, 2, BS, nz_dev)
    planes = pairs[:, :, 0] + pairs[:, :, 1]
    means = 0.125 * exact_dot(
        "ay,fxyl,lm->fxam", replicate(half, BS), planes, replicate(nblk * half, nz_dev).T
    )
    means = means.reshape(5, half, half, nblk, half)
    return means.transpose(3, 0, 1, 2, 4).reshape(nblk, -1)


def pick(table, index):
    flat = table.reshape((-1,) + table.shape[2:])
    return jnp.take(flat, index.reshape(-1), axis=0, mode="clip").reshape(
        index.shape + table.shape[2:]
    )


def select(mask, value):
    return jnp.sum(jnp.where(mask, value, 0), axis=-1)


def shards(fine, shell, parent, link):
    nz_dev = fine.shape[3]
    nblk = nz_dev // BS
    rows = lax.axis_size("gy")
    cols = lax.axis_size("gz")
    my = lax.axis_index("gy")
    mz = lax.axis_index("gz")
    me = my * cols + mz
    parent_row = parent[0]
    count = parent_row.shape[0]
    links = link[:, 0, 0, :].T
    width = shell.shape[2] // 2

    item = jnp.arange(count, dtype=jnp.int32)
    dev = item // nblk
    d_row = dev // cols
    d_col = dev % cols
    owner = parent_row // nblk
    slot = parent_row % nblk
    o_row = owner // cols
    o_col = owner % cols
    before = item[None, :] < item[:, None]
    rank1 = jnp.sum(
        (before & (owner[None, :] == owner[:, None]) & (d_row[None, :] == d_row[:, None])).astype(
            jnp.int32
        ),
        axis=1,
    )
    rank2 = jnp.sum(
        (before & (dev[None, :] == dev[:, None]) & (o_col[None, :] == o_col[:, None])).astype(
            jnp.int32
        ),
        axis=1,
    )
    peer_r = jnp.arange(rows, dtype=jnp.int32)[:, None, None]
    peer_c = jnp.arange(cols, dtype=jnp.int32)[:, None, None]
    cell = jnp.arange(nblk, dtype=jnp.int32)[None, :, None]
    via_me = (d_row == my) & (o_col == mz)

    local = shell[0]
    levels = jnp.concatenate(
        [local[:, :width], 0.5 * (local[:, :width] + local[:, width:])], axis=1
    )
    first = select((owner == me) & (d_row == peer_r) & (rank1 == cell), slot)
    stage = lax.all_to_all(pick(levels[None], first), "gy", 0, 0, tiled=True)
    second = select(via_me & (d_col == peer_c) & (rank2 == cell), o_row * nblk + rank1)
    stage = lax.all_to_all(pick(stage, second), "gz", 0, 0, tiled=True)
    mine = lax.dynamic_slice_in_dim(item, me * nblk, nblk)
    fetched = pick(stage, o_col[mine] * nblk + rank2[mine])

    state = fine
    for step in range(2):
        side, ends = coarse_faces(fetched[:, step * width : (step + 1) * width], nblk)
        state = substep(state, *ghost_inputs(state, side[0], ends[0], links))
    restricted = restrict_state(state, nblk)

    pos = jnp.arange(nblk, dtype=jnp.int32)
    back = select(
        (o_col[mine][None, None, :] == peer_c) & (rank2[mine][None, None, :] == cell), pos
    )
    stage = lax.all_to_all(pick(restricted[None], back), "gz", 0, 0, tiled=True)
    home = select(via_me & (o_row == peer_r) & (rank1 == cell), d_col * nblk + rank2)
    stage = lax.all_to_all(pick(stage, home), "gy", 0, 0, tiled=True)
    target = me * nblk + pos
    origin = select(parent_row[None, :] == target[:, None], d_row * nblk + rank1)
    coarse_new = pick(stage, origin).reshape(1, nblk, restricted.shape[1])
    return (state, coarse_new)


def solution(mesh):
    return jax.shard_map(
        shards,
        mesh=mesh,
        in_specs=(
            P(None, "gx", "gy", "gz"),
            P("gx", ("gy", "gz"), None),
            P("gx", None),
            P(None, "gx", "gy", "gz"),
        ),
        out_specs=(P(None, "gx", "gy", "gz"), P("gx", ("gy", "gz"), None)),
        check_vma=False,
    )
```

```python
import jax
import jax.numpy as jnp
from jax import lax
from jax.experimental import pallas as pl
from jax.experimental.pallas import tpu as pltpu
from jax.sharding import PartitionSpec as P

BS = 16

GAMMA = 1.4
LAMBDA = 0.05


def shift_in(plane, axis, forward):
    count = lax.axis_size(axis)
    if forward:
        pairs = [(i, (i + 1) % count) for i in range(count)]
    else:
        pairs = [((i + 1) % count, i) for i in range(count)]
    return lax.ppermute(plane, axis, pairs)


def prims(v):
    rho, mx, my, mz, energy = v
    ux = mx / rho
    uy = my / rho
    uz = mz / rho
    press = (GAMMA - 1.0) * (energy - 0.5 * (mx * ux + my * uy + mz * uz))
    sound = jnp.sqrt(GAMMA * press / rho)
    return (ux, uy, uz), press, sound


def flux_of(v, prim, direc):
    rho, mx, my, mz, energy = v
    vel, press, sound = prim
    normal = vel[direc]
    mom = (mx, my, mz)
    parts = [mom[direc], mx * normal, my * normal, mz * normal, (energy + press) * normal]
    parts[1 + direc] = parts[1 + direc] + press
    return parts, jnp.abs(normal) + sound


def face_of(fa, sa, va, fb, sb, vb):
    wave = 0.5 * jnp.maximum(sa, sb)
    return [0.5 * (fa[i] + fb[i]) - wave * (vb[i] - va[i]) for i in range(5)]


def substep_kernel(u_ref, gx_ref, gy_ref, zfix_ref, zflag_ref, o_ref):
    nx = u_ref.shape[1]
    ny = u_ref.shape[2]
    nz = u_ref.shape[3]
    row = lax.broadcasted_iota(jnp.int32, (ny, nz), 0)
    over_lo = zflag_ref[0] != 0
    over_hi = zflag_ref[1] != 0

    def body(x, carry):
        cen = [u_ref[f, x] for f in range(5)]
        below = jnp.maximum(x - 1, 0)
        above = jnp.minimum(x + 1, nx - 1)
        xm = [jnp.where(x == 0, gx_ref[0, f], u_ref[f, below]) for f in range(5)]
        xp = [jnp.where(x == nx - 1, gx_ref[1, f], u_ref[f, above]) for f in range(5)]
        ym = [
            jnp.where(row == 0, jnp.broadcast_to(gy_ref[0, x, f], (ny, nz)), pltpu.roll(cen[f], 1, 0))
            for f in range(5)
        ]
        yp = [
            jnp.where(
                row == ny - 1, jnp.broadcast_to(gy_ref[1, x, f], (ny, nz)), pltpu.roll(cen[f], ny - 1, 0)
            )
            for f in range(5)
        ]
        zm = [jnp.where(over_lo, zfix_ref[f, x], pltpu.roll(cen[f], 1, 1)) for f in range(5)]
        zp = [jnp.where(over_hi, zfix_ref[f, x], pltpu.roll(cen[f], nz - 1, 1)) for f in range(5)]
        pc = prims(cen)
        total = None
        for direc, (lo, hi) in enumerate(((xm, xp), (ym, yp), (zm, zp))):
            fc, sc = flux_of(cen, pc, direc)
            fl, sl = flux_of(lo, prims(lo), direc)
            fh, sh = flux_of(hi, prims(hi), direc)
            left = face_of(fl, sl, lo, fc, sc, cen)
            right = face_of(fc, sc, cen, fh, sh, hi)
            diff = [right[i] - left[i] for i in range(5)]
            total = diff if total is None else [total[i] + diff[i] for i in range(5)]
        for f in range(5):
            o_ref[f, x] = cen[f] - LAMBDA * total[f]
        return carry

    lax.fori_loop(0, nx, body, 0)


def substep(state, gx, gy, zfix, zflag):
    return pl.pallas_call(
        substep_kernel, out_shape=jax.ShapeDtypeStruct(state.shape, state.dtype)
    )(state, gx, gy, zfix, zflag)


def replicate(rows, cols):
    step = cols // rows
    return (jnp.arange(cols)[None, :] // step == jnp.arange(rows)[:, None]).astype(jnp.float32)


def exact_dot(spec, *ops):
    return jnp.einsum(spec, *ops, precision=lax.Precision.HIGHEST, preferred_element_type=jnp.float32)


def coarse_faces(fetched, nblk):
    half = BS // 2
    lv = fetched.reshape(nblk, 2, 6, 5, half, half)
    rows = replicate(half, BS)
    side = lv[:, :, 0:4].transpose(1, 2, 3, 4, 0, 5).reshape(2, 4, 5, half, nblk * half)
    side = exact_dot("ay,lkfab,bz->lkfyz", rows, side, replicate(nblk * half, nblk * BS))
    ends = lv[:, :, 4:6].transpose(1, 2, 3, 4, 5, 0)
    lane = jnp.arange(nblk * BS)
    starts = (lane % BS == 0)[None, :]
    spread = replicate(nblk, nblk * BS)
    choose = jnp.stack([jnp.where(starts, spread, 0.0), jnp.where(starts, 0.0, spread)])
    ends = exact_dot("ax,by,lkfabc,kcz->lfxyz", rows, rows, ends, choose)
    return side, ends


def ghost_inputs(state, side, ends, links):
    nz_dev = state.shape[3]
    chosen = [jnp.repeat(links[:, face] == 1, BS)[None, None, :] for face in range(4)]
    gx = jnp.stack(
        [
            jnp.where(chosen[0], shift_in(state[:, -1], "gx", True), side[0]),
            jnp.where(chosen[1], shift_in(state[:, 0], "gx", False), side[1]),
        ]
    )
    gy = jnp.stack(
        [
            jnp.where(chosen[2], shift_in(state[:, :, -1], "gy", True), side[2]),
            jnp.where(chosen[3], shift_in(state[:, :, 0], "gy", False), side[3]),
        ]
    )
    gy = gy.transpose(0, 2, 1, 3)[:, :, :, None, :]
    far_lo = shift_in(state[..., -1], "gz", True)
    far_hi = shift_in(state[..., 0], "gz", False)
    lane = jnp.arange(nz_dev, dtype=jnp.int32)
    at_lo = lane % BS == 0
    at_hi = lane % BS == BS - 1
    link_lo = jnp.repeat(links[:, 4] == 1, BS)
    link_hi = jnp.repeat(links[:, 5] == 1, BS)
    zfix = jnp.where(
        link_lo & (lane == 0),
        far_lo[..., None],
        jnp.where(link_hi & (lane == nz_dev - 1), far_hi[..., None], ends),
    )
    flag_lo = at_lo & (~link_lo | (lane == 0))
    flag_hi = at_hi & (~link_hi | (lane == nz_dev - 1))
    zflag = jnp.broadcast_to(
        jnp.stack([flag_lo, flag_hi]).astype(jnp.int32)[:, None, :], (2, state.shape[2], nz_dev)
    )
    return gx, gy, zfix, zflag


def restrict_state(state, nblk):
    half = BS // 2
    nz_dev = state.shape[3]
    pairs = state.reshape(5, half, 2, BS, nz_dev)
    planes = pairs[:, :, 0] + pairs[:, :, 1]
    means = 0.125 * exact_dot(
        "ay,fxyl,lm->fxam", replicate(half, BS), planes, replicate(nblk * half, nz_dev).T
    )
    means = means.reshape(5, half, half, nblk, half)
    return means.transpose(3, 0, 1, 2, 4).reshape(nblk, -1)


def pick(table, index):
    flat = table.reshape((-1,) + table.shape[2:])
    return jnp.take(flat, index.reshape(-1), axis=0, mode="clip").reshape(
        index.shape + table.shape[2:]
    )


def select(mask, value):
    return jnp.sum(jnp.where(mask, value, 0), axis=-1)


def shards(fine, shell, parent, link):
    nz_dev = fine.shape[3]
    nblk = nz_dev // BS
    rows = lax.axis_size("gy")
    cols = lax.axis_size("gz")
    my = lax.axis_index("gy")
    mz = lax.axis_index("gz")
    me = my * cols + mz
    parent_row = parent[0]
    count = parent_row.shape[0]
    links = link[:, 0, 0, :].T
    width = shell.shape[2] // 2

    item = jnp.arange(count, dtype=jnp.int32)
    dev = item // nblk
    d_row = dev // cols
    d_col = dev % cols
    owner = parent_row // nblk
    slot = parent_row % nblk
    o_row = owner // cols
    o_col = owner % cols
    before = item[None, :] < item[:, None]
    rank1 = jnp.sum(
        (before & (owner[None, :] == owner[:, None]) & (d_row[None, :] == d_row[:, None])).astype(
            jnp.int32
        ),
        axis=1,
    )
    cols_of = o_col.reshape(-1, nblk)
    pos = jnp.arange(nblk, dtype=jnp.int32)
    rank2 = jnp.sum(
        (
            (pos[None, :] < pos[:, None])[None] & (cols_of[:, :, None] == cols_of[:, None, :])
        ).astype(jnp.int32),
        axis=2,
    ).reshape(-1)
    peer_r = jnp.arange(rows, dtype=jnp.int32)[:, None, None]
    peer_c = jnp.arange(cols, dtype=jnp.int32)[:, None, None]
    cell = jnp.arange(nblk, dtype=jnp.int32)[None, :, None]
    via_me = (d_row == my) & (o_col == mz)

    local = shell[0]
    levels = jnp.concatenate(
        [local[:, :width], 0.5 * (local[:, :width] + local[:, width:])], axis=1
    )
    first = select((owner == me) & (d_row == peer_r) & (rank1 == cell), slot)
    stage = lax.all_to_all(pick(levels[None], first), "gy", 0, 0, tiled=True)
    second = select(via_me & (d_col == peer_c) & (rank2 == cell), o_row * nblk + rank1)
    stage = lax.all_to_all(pick(stage, second), "gz", 0, 0, tiled=True)
    mine = lax.dynamic_slice_in_dim(item, me * nblk, nblk)
    fetched = pick(stage, o_col[mine] * nblk + rank2[mine])

    side, ends = coarse_faces(fetched, nblk)
    state = fine
    for step in range(2):
        state = substep(state, *ghost_inputs(state, side[step], ends[step], links))
    restricted = restrict_state(state, nblk)

    pos = jnp.arange(nblk, dtype=jnp.int32)
    back = select(
        (o_col[mine][None, None, :] == peer_c) & (rank2[mine][None, None, :] == cell), pos
    )
    stage = lax.all_to_all(pick(restricted[None], back), "gz", 0, 0, tiled=True)
    home = select(via_me & (o_row == peer_r) & (rank1 == cell), d_col * nblk + rank2)
    stage = lax.all_to_all(pick(stage, home), "gy", 0, 0, tiled=True)
    target = me * nblk + pos
    origin = select(parent_row[None, :] == target[:, None], d_row * nblk + rank1)
    coarse_new = pick(stage, origin).reshape(1, nblk, restricted.shape[1])
    return (state, coarse_new)


def solution(mesh):
    return jax.shard_map(
        shards,
        mesh=mesh,
        in_specs=(
            P(None, "gx", "gy", "gz"),
            P("gx", ("gy", "gz"), None),
            P("gx", None),
            P(None, "gx", "gy", "gz"),
        ),
        out_specs=(P(None, "gx", "gy", "gz"), P("gx", ("gy", "gz"), None)),
        check_vma=False,
    )
```
